128 devices in a mesh: grp: 4 (over y), dev: 32 (over z, x, core).
Axes of the slice: x: 4, y: 4, z: 4, core: 2. Of those that a mesh axis runs over, the one named last changes fastest.
Arguments:
- ref_volume: bfloat16 [1024, 128, 1024], P('dev', None, 'grp'), may hold values from -6 to 6
- def_volume: bfloat16 [1024, 128, 1024], P('dev', None, 'grp'), may hold values from -6 to 6
- shifts: int32 [4, 32], P('grp', 'dev'), may hold values from -8 to 8, as said below
- init_disp: float32 [3, 65, 9, 65], replicated, may hold values from -3 to 3
- precond: float32 [3, 65, 9, 65], replicated, may hold values from 0.001 to 0.01
Outputs:
- displacement: float32 [3, 65, 9, 65], replicated
- residual: float32 [1024, 128, 1024], P('dev', None, 'grp')
- misfit: float32 [], replicated
The draws below stay inside these ranges and needn't reach their ends.
Inputs may be any that keep to these rules, and one draw needn't show every extreme that they name: `shifts`: every entry lies within 8 in magnitude; both 8 and -8 occur in every draw.
All inputs are finite; a program needn't handle non-finite values.
Results may differ from the reference program's by a relative error of at most 0.0003.
Values may be sent and summed in bfloat16 or wider, within the bound.
No kernel may reach another device: no remote copies, remote signals or barrier semaphores. Data moves between devices by JAX's collectives and lax.ppermute only.
A program may use at most 128 MiB of HBM per device.

```python
import math
import jax
import jax.numpy as jnp
from jax import lax

E = 16
SMAX = 8
ITERS = 2
BX = 32
YW = 128
BZ = 256
GROUPS = 4
BRICKS = 32
NX = 1024
NZ = 1024
NODES_X = 65
NODES_Y = 9
NODES_Z = 65
NODES_BX = 3
NODES_BZ = 17


def draw_shifts(key, part):
    base = jax.random.randint(jax.random.fold_in(key, 11), (GROUPS * BRICKS,), -SMAX, SMAX + 1)
    order = jax.random.permutation(jax.random.fold_in(key, 12), GROUPS * BRICKS)
    base = base.at[order[0]].set(SMAX)
    base = base.at[order[1]].set(-SMAX)
    return base.reshape(GROUPS, BRICKS).astype(jnp.int32)


def rising_scale(key):
    along_x = (jnp.arange(NX, dtype=jnp.float32) + 0.5) / NX
    along_z = (jnp.arange(NZ, dtype=jnp.float32) + 0.5) / NZ
    extra_x = jnp.zeros((), jnp.float32)
    extra_z = jnp.zeros((), jnp.float32)
    grow_x = jnp.exp((1.0986123 + extra_x) * along_x)
    grow_z = jnp.exp((1.0986123 + extra_z) * along_z)
    return grow_x[:, None, None] * grow_z[None, None, :]


def textured(key, salt):
    shape = (NX, YW, NZ)
    cells = (NX // 8, YW // 8, NZ // 8)
    base = jax.random.truncated_normal(jax.random.fold_in(key, salt + 3), -3.5, 3.5, shape, jnp.float32)
    level = jax.random.uniform(jax.random.fold_in(key, salt + 4), cells, jnp.float32, -0.4, 0.4)
    start = 0.45
    mixed = (base + jnp.roll(base, (1, 1), axis=(0, 1))) * 0.70710678
    amplitude = jnp.exp(level)
    amplitude = jnp.repeat(jnp.repeat(jnp.repeat(amplitude, 8, axis=0), 8, axis=1), 8, axis=2)
    scale = start * rising_scale(key)
    return jnp.clip(mixed * amplitude * scale, -6.0, 6.0).astype(jnp.bfloat16)


def draw_def_volume(key, part):
    return textured(key, 20)


def draw_ref_volume(key, part):
    return textured(key, 40)


def draw_init_disp(key, part):
    shape = (NODES_X, NODES_Y, NODES_Z)
    common = 0.4 * jax.random.normal(jax.random.fold_in(key, 35), shape, jnp.float32)
    noise_x = 0.3 * jax.random.normal(jax.random.fold_in(key, 36), shape, jnp.float32)
    noise_y = 0.3 * jax.random.normal(jax.random.fold_in(key, 37), shape, jnp.float32)
    along_z = 0.5 * jax.random.normal(jax.random.fold_in(key, 38), shape, jnp.float32)
    stacked = jnp.stack([common + noise_x, noise_y - common, along_z])
    return jnp.clip(stacked, -3.0, 3.0).astype(jnp.float32)


def setup_inputs(seed: int = 0) -> dict:
    arg_keys = jax.random.split(jax.random.key(seed), 6)
    ref_volume = draw_ref_volume(jax.random.fold_in(arg_keys[5], 71), 0)
    def_volume = draw_def_volume(jax.random.fold_in(arg_keys[5], 71), 0)
    shifts = draw_shifts(jax.random.fold_in(arg_keys[5], 71), 0)
    init_disp = draw_init_disp(jax.random.fold_in(arg_keys[5], 71), 0)
    precond = jnp.clip(jnp.exp(jax.random.uniform(arg_keys[4], (3, NODES_X, NODES_Y, NODES_Z), jnp.float32, math.log(0.001), math.log(0.01))), 0.001, 0.01)
    return {"ref_volume": ref_volume, "def_volume": def_volume, "shifts": shifts, "init_disp": init_disp, "precond": precond}


epsilon = 1e-06

def hat_matrix(voxels, nodes):
    positions = jnp.arange(voxels, dtype=jnp.int32)
    element = positions // E
    fraction = (positions - element * E).astype(jnp.float32) / E
    columns = jnp.arange(nodes, dtype=jnp.int32)
    left_part = (columns[None, :] == element[:, None]).astype(jnp.float32) * (1.0 - fraction)[:, None]
    right_part = (columns[None, :] == element[:, None] + 1).astype(jnp.float32) * fraction[:, None]
    return left_part + right_part

def smooth(values, direction):
    extent = values.shape[direction]
    lower = lax.slice_in_dim(values, 0, extent - 2, axis=direction)
    middle = lax.slice_in_dim(values, 1, extent - 1, axis=direction)
    upper = lax.slice_in_dim(values, 2, extent, axis=direction)
    return (lower + 4.0 * middle + upper) / 6.0

def differ(values, direction):
    extent = values.shape[direction]
    lower = lax.slice_in_dim(values, 0, extent - 2, axis=direction)
    upper = lax.slice_in_dim(values, 2, extent, axis=direction)
    return 0.5 * (upper - lower)

def gradients(window):
    smooth_z = smooth(window, 2)
    slope_x = differ(smooth(smooth_z, 1), 0)
    slope_y = smooth(differ(smooth_z, 1), 0)
    slope_z = smooth(smooth(differ(window, 2), 1), 0)
    return jnp.stack([slope_x, slope_y, slope_z])

def interpolate(local_nodes, hat_x, hat_y, hat_z):
    highest = lax.Precision.HIGHEST
    partial_z = jnp.einsum('cijk,zk->cijz', local_nodes, hat_z, precision=highest)
    partial_y = jnp.einsum('cijz,yj->ciyz', partial_z, hat_y, precision=highest)
    return jnp.einsum('ciyz,xi->cxyz', partial_y, hat_x, precision=highest)

def restrict(terms, hat_x, hat_y, hat_z):
    highest = lax.Precision.HIGHEST
    partial_x = jnp.einsum('cxyz,xi->ciyz', terms, hat_x, precision=highest)
    partial_y = jnp.einsum('ciyz,yj->cijz', partial_x, hat_y, precision=highest)
    return jnp.einsum('cijz,zk->cijk', partial_y, hat_z, precision=highest)

def reference(ref_volume, def_volume, shifts, init_disp, precond):
    margin = SMAX + 1
    padded = jnp.pad(def_volume, ((margin, margin), (1, 1), (1, 1)))
    voxel_count = float(NX * YW * NZ)
    target_all = ref_volume.astype(jnp.float32)
    mean_ref = jnp.sum(target_all) / voxel_count
    var_ref = jnp.sum(target_all * target_all) / voxel_count - mean_ref * mean_ref
    hat_x = hat_matrix(BX, NODES_BX)
    hat_y = hat_matrix(YW, NODES_Y)
    hat_z = hat_matrix(BZ, NODES_BZ)
    brick_ids = jnp.arange(GROUPS * BRICKS, dtype=jnp.int32)
    zero_index = jnp.zeros((), jnp.int32)

    def corner_of(brick):
        group_index = (brick // BRICKS).astype(jnp.int32)
        brick_index = (brick % BRICKS).astype(jnp.int32)
        return (group_index, brick_index)

    def state(motion, brick):
        group_index, brick_index = corner_of(brick)
        offset = shifts[group_index, brick_index].astype(jnp.int32)
        start_x = (brick_index * BX + offset + margin - 1).astype(jnp.int32)
        start_z = (group_index * BZ).astype(jnp.int32)
        window = lax.dynamic_slice(padded, (start_x, zero_index, start_z), (BX + 2, YW + 2, BZ + 2)).astype(jnp.float32)
        slopes = gradients(window)
        sample = window[1:-1, 1:-1, 1:-1]
        node_x = (brick_index * (BX // E)).astype(jnp.int32)
        node_z = (group_index * (BZ // E)).astype(jnp.int32)
        local_nodes = lax.dynamic_slice(motion, (zero_index, node_x, zero_index, node_z), (3, NODES_BX, NODES_Y, NODES_BZ))
        shift_field = interpolate(local_nodes, hat_x, hat_y, hat_z)
        warped = sample + lax.optimization_barrier(jnp.sum(shift_field * slopes, axis=0))
        target = lax.dynamic_slice(ref_volume, ((brick_index * BX).astype(jnp.int32), zero_index, start_z), (BX, YW, BZ)).astype(jnp.float32)
        return (warped, slopes, target)
    motion = init_disp
    residuals = None
    squares = None
    for iteration in range(ITERS):

        def moments(brick):
            warped, slopes, target = state(motion, brick)
            return jnp.stack([jnp.sum(warped), jnp.sum(warped * warped)])
        totals = lax.optimization_barrier(jnp.sum(lax.map(moments, brick_ids), axis=0))
        mean_img = totals[0] / voxel_count
        var_img = totals[1] / voxel_count - mean_img * mean_img
        ratio = jnp.sqrt((var_ref + epsilon) / (var_img + epsilon))

        def forces_of(brick):
            warped, slopes, target = state(motion, brick)
            residual_brick = target - mean_ref - ratio * (warped - mean_img)
            slab = restrict(slopes * residual_brick[None], hat_x, hat_y, hat_z)
            return (slab, residual_brick, jnp.sum(residual_brick * residual_brick))
        slabs, residuals, squares = lax.map(forces_of, brick_ids)

        def add_slab(brick, total):
            group_index, brick_index = corner_of(brick)
            corner = (zero_index, (brick_index * (BX // E)).astype(jnp.int32), zero_index, (group_index * (BZ // E)).astype(jnp.int32))
            current = lax.dynamic_slice(total, corner, (3, NODES_BX, NODES_Y, NODES_BZ))
            return lax.dynamic_update_slice(total, current + slabs[brick], corner)
        forces = lax.fori_loop(jnp.int32(0), jnp.int32(GROUPS * BRICKS), add_slab, jnp.zeros((3, NODES_X, NODES_Y, NODES_Z), jnp.float32))
        motion = motion + precond * forces
    residual_field = residuals.reshape(GROUPS, BRICKS, BX, YW, BZ).transpose(1, 2, 3, 0, 4).reshape(NX, YW, NZ)
    misfit = jnp.sqrt(jnp.sum(squares) / voxel_count)
    return (motion, residual_field, misfit)
```

```python
import jax
import jax.numpy as jnp
from jax import lax
from jax.sharding import PartitionSpec as P

E = 16
SMAX = 8
ITERS = 2


epsilon = 1e-06


def with_halo(shard, sides, width):
    for axis, dim in sides:
        devices, length = (lax.axis_size(axis), shard.shape[dim])
        up = [(i, (i + 1) % devices) for i in range(devices - 1)]
        down = [(j, i) for i, j in up]
        last = lax.slice_in_dim(shard, length - width, length, axis=dim)
        initial = lax.slice_in_dim(shard, 0, width, axis=dim)
        before = lax.ppermute(last, axis, up)
        after = lax.ppermute(initial, axis, down)
        shard = jnp.concatenate([before, shard, after], axis=dim)
    return shard


def hat_matrix(voxels, nodes):
    positions = jnp.arange(voxels, dtype=jnp.int32)
    element = positions // E
    fraction = (positions - element * E).astype(jnp.float32) / E
    columns = jnp.arange(nodes, dtype=jnp.int32)
    left_part = (columns[None, :] == element[:, None]).astype(jnp.float32) * (1.0 - fraction)[
        :, None
    ]
    right_part = (columns[None, :] == element[:, None] + 1).astype(jnp.float32) * fraction[:, None]
    return left_part + right_part


def smooth(values, direction):
    extent = values.shape[direction]
    lower = lax.slice_in_dim(values, 0, extent - 2, axis=direction)
    middle = lax.slice_in_dim(values, 1, extent - 1, axis=direction)
    upper = lax.slice_in_dim(values, 2, extent, axis=direction)
    return (lower + 4.0 * middle + upper) / 6.0


def differ(values, direction):
    extent = values.shape[direction]
    lower = lax.slice_in_dim(values, 0, extent - 2, axis=direction)
    upper = lax.slice_in_dim(values, 2, extent, axis=direction)
    return 0.5 * (upper - lower)


def gradients(window):
    smooth_z = smooth(window, 2)
    slope_x = differ(smooth(smooth_z, 1), 0)
    slope_y = smooth(differ(smooth_z, 1), 0)
    slope_z = smooth(smooth(differ(window, 2), 1), 0)
    return jnp.stack([slope_x, slope_y, slope_z])


def interpolate(local_nodes, hat_x, hat_y, hat_z):
    highest = lax.Precision.HIGHEST
    partial_z = jnp.einsum("cijk,zk->cijz", local_nodes, hat_z, precision=highest)
    partial_y = jnp.einsum("cijz,yj->ciyz", partial_z, hat_y, precision=highest)
    return jnp.einsum("ciyz,xi->cxyz", partial_y, hat_x, precision=highest)


def restrict(terms, hat_x, hat_y, hat_z):
    highest = lax.Precision.HIGHEST
    partial_x = jnp.einsum("cxyz,xi->ciyz", terms, hat_x, precision=highest)
    partial_y = jnp.einsum("ciyz,yj->cijz", partial_x, hat_y, precision=highest)
    return jnp.einsum("cijz,zk->cijk", partial_y, hat_z, precision=highest)


def allsum(values):
    for axis in ("dev", "grp"):
        devices = lax.axis_size(axis)
        assert devices & (devices - 1) == 0
        step = 1
        while step < devices:
            pairs = [(i, i ^ step) for i in range(devices)]
            values = values + lax.ppermute(values, axis, pairs)
            step *= 2
    return values


def share_nodes(slab):
    for axis, dim in (("dev", 1), ("grp", 3)):
        devices, length = (lax.axis_size(axis), slab.shape[dim])
        up = [(i, i + 1) for i in range(devices - 1)]
        down = [(j, i) for i, j in up]
        last = lax.index_in_dim(slab, length - 1, axis=dim, keepdims=False)
        first = lax.index_in_dim(slab, 0, axis=dim, keepdims=False)
        before = lax.ppermute(last, axis, up)
        after = lax.ppermute(first, axis, down)
        head = lax.index_in_dim(slab, 0, axis=dim) + jnp.expand_dims(before, dim)
        tail = lax.index_in_dim(slab, length - 1, axis=dim) + jnp.expand_dims(after, dim)
        middle = lax.slice_in_dim(slab, 1, length - 1, axis=dim)
        slab = jnp.concatenate([head, middle, tail], axis=dim)
    return slab


def assemble(gathered):
    groups, bricks, comps, nbx, nby, nbz = gathered.shape
    ex, ez = nbx - 1, nbz - 1
    main = gathered[:, :, :, :ex].transpose(0, 2, 1, 3, 4, 5)
    main = main.reshape(groups, comps, bricks * ex, nby, nbz)
    main = jnp.pad(main, ((0, 0), (0, 0), (0, 1), (0, 0), (0, 0)))
    edge = gathered[:, :, :, ex].transpose(0, 2, 1, 3, 4)[:, :, :, None]
    edge = jnp.pad(edge, ((0, 0), (0, 0), (1, 0), (0, ex - 1), (0, 0), (0, 0)))
    edge = edge.reshape(groups, comps, (bricks + 1) * ex, nby, nbz)[:, :, : bricks * ex + 1]
    along_x = main + edge
    main = along_x[..., :ez].transpose(1, 2, 3, 0, 4)
    main = main.reshape(comps, bricks * ex + 1, nby, groups * ez)
    main = jnp.pad(main, ((0, 0), (0, 0), (0, 0), (0, 1)))
    edge = along_x[..., ez].transpose(1, 2, 3, 0)[..., None]
    edge = jnp.pad(edge, ((0, 0), (0, 0), (0, 0), (1, 0), (0, ez - 1)))
    edge = edge.reshape(comps, bricks * ex + 1, nby, (groups + 1) * ez)[..., : groups * ez + 1]
    return main + edge


def local(ref_volume, def_volume, shifts, init_disp, precond):
    width_x, rows_y, depth_z = ref_volume.shape
    dev_count = lax.axis_size("dev")
    grp_count = lax.axis_size("grp")
    grp_index = lax.axis_index("grp")
    dev_index = lax.axis_index("dev")
    voxel_count = float(width_x * rows_y * depth_z * dev_count * grp_count)
    margin = SMAX + 1
    offset = shifts[0, 0]
    widened = with_halo(def_volume, (("dev", 0),), margin)
    framed = with_halo(widened, (("grp", 2),), 1)
    window = lax.dynamic_slice_in_dim(framed, offset + margin - 1, width_x + 2, 0)
    window = jnp.pad(window, ((0, 0), (1, 1), (0, 0))).astype(jnp.float32)
    slopes = gradients(window)
    sample = window[1:-1, 1:-1, 1:-1]
    target = ref_volume.astype(jnp.float32)
    elements_x = width_x // E
    elements_z = depth_z // E
    nodes_y = rows_y // E + 1
    hat_x = hat_matrix(width_x, elements_x + 1)
    hat_y = hat_matrix(rows_y, nodes_y)
    hat_z = hat_matrix(depth_z, elements_z + 1)
    corner = (0, dev_index * elements_x, 0, grp_index * elements_z)
    extent = (3, elements_x + 1, nodes_y, elements_z + 1)
    local_nodes = lax.dynamic_slice(init_disp, corner, extent)
    local_precond = lax.dynamic_slice(precond, corner, extent)
    target_sums = jnp.stack([jnp.sum(target), jnp.sum(target * target)])
    residual = target
    total_slab = None
    mean_ref = var_ref = None
    for iteration in range(ITERS):
        shift_field = interpolate(local_nodes, hat_x, hat_y, hat_z)
        warped = sample + jnp.sum(shift_field * slopes, axis=0)
        image_sums = jnp.stack([jnp.sum(warped), jnp.sum(warped * warped)])
        if iteration == 0:
            sums = allsum(jnp.concatenate([target_sums, image_sums]))
            mean_ref = sums[0] / voxel_count
            var_ref = sums[1] / voxel_count - mean_ref * mean_ref
            image_sums = sums[2:]
        else:
            image_sums = allsum(image_sums)
        mean_img = image_sums[0] / voxel_count
        var_img = image_sums[1] / voxel_count - mean_img * mean_img
        ratio = jnp.sqrt((var_ref + epsilon) / (var_img + epsilon))
        residual = target - mean_ref - ratio * (warped - mean_img)
        slab = restrict(slopes * residual[None], hat_x, hat_y, hat_z)
        total_slab = slab if total_slab is None else total_slab + slab
        if iteration + 1 < ITERS:
            local_nodes = local_nodes + local_precond * share_nodes(slab)
    squares = jnp.sum(residual * residual)
    packed = jnp.concatenate([total_slab.reshape(-1), squares[None]])
    gathered = lax.all_gather(packed.reshape(2, -1), ("grp", "dev")).reshape(grp_count * dev_count, -1)
    pieces = gathered[:, :-1].reshape((grp_count, dev_count) + total_slab.shape)
    forces = assemble(pieces)
    motion = init_disp + precond * forces
    misfit = jnp.sqrt(jnp.sum(gathered[:, -1]) / voxel_count)
    return (motion, residual, misfit)


def solution(mesh):
    placed = (P("dev", None, "grp"), P("dev", None, "grp"), P("grp", "dev"), P(), P())
    return jax.shard_map(
        local,
        mesh=mesh,
        in_specs=placed,
        out_specs=(P(), P("dev", None, "grp"), P()),
        check_vma=False,
    )
```

```python
import jax
import jax.numpy as jnp
from jax import lax
from jax.sharding import PartitionSpec as P

E = 16
SMAX = 8
ITERS = 2


epsilon = 1e-06


def with_halo(shard, sides, width):
    for axis, dim in sides:
        devices, length = (lax.axis_size(axis), shard.shape[dim])
        up = [(i, (i + 1) % devices) for i in range(devices - 1)]
        down = [(j, i) for i, j in up]
        last = lax.slice_in_dim(shard, length - width, length, axis=dim)
        initial = lax.slice_in_dim(shard, 0, width, axis=dim)
        before = lax.ppermute(last, axis, up)
        after = lax.ppermute(initial, axis, down)
        shard = jnp.concatenate([before, shard, after], axis=dim)
    return shard


def hat_matrix(voxels, nodes):
    positions = jnp.arange(voxels, dtype=jnp.int32)
    element = positions // E
    fraction = (positions - element * E).astype(jnp.float32) / E
    columns = jnp.arange(nodes, dtype=jnp.int32)
    left_part = (columns[None, :] == element[:, None]).astype(jnp.float32) * (1.0 - fraction)[
        :, None
    ]
    right_part = (columns[None, :] == element[:, None] + 1).astype(jnp.float32) * fraction[:, None]
    return left_part + right_part


def smooth(values, direction):
    extent = values.shape[direction]
    lower = lax.slice_in_dim(values, 0, extent - 2, axis=direction)
    middle = lax.slice_in_dim(values, 1, extent - 1, axis=direction)
    upper = lax.slice_in_dim(values, 2, extent, axis=direction)
    return (lower + 4.0 * middle + upper) / 6.0


def differ(values, direction):
    extent = values.shape[direction]
    lower = lax.slice_in_dim(values, 0, extent - 2, axis=direction)
    upper = lax.slice_in_dim(values, 2, extent, axis=direction)
    return 0.5 * (upper - lower)


def gradients(window):
    smooth_z = smooth(window, 2)
    slope_x = differ(smooth(smooth_z, 1), 0)
    slope_y = smooth(differ(smooth_z, 1), 0)
    slope_z = smooth(smooth(differ(window, 2), 1), 0)
    return jnp.stack([slope_x, slope_y, slope_z])


def interpolate(local_nodes, hat_y, hat_z):
    highest = lax.Precision.HIGHEST
    partial_z = jnp.einsum("cijk,zk->cijz", local_nodes, hat_z, precision=highest)
    return jnp.einsum("cijz,yj->ciyz", partial_z, hat_y, precision=highest)


def expand_x(partial_y, hat_x):
    return sum(
        hat_x[None, :, i, None, None] * partial_y[:, i, None] for i in range(hat_x.shape[1])
    )


def restrict(terms, hat_x, hat_y, hat_z):
    highest = lax.Precision.HIGHEST
    partial_x = jnp.stack(
        [jnp.sum(terms * hat_x[None, :, i, None, None], axis=1) for i in range(hat_x.shape[1])],
        axis=1,
    )
    partial_y = jnp.einsum("ciyz,yj->cijz", partial_x, hat_y, precision=highest)
    return jnp.einsum("cijz,zk->cijk", partial_y, hat_z, precision=highest)


def scatter_matrix(bricks, elements):
    columns = jnp.arange(bricks * elements + 1, dtype=jnp.int32)
    starts = jnp.arange(bricks, dtype=jnp.int32)[:, None] * elements
    rows = starts + jnp.arange(elements + 1, dtype=jnp.int32)[None, :]
    return (rows[:, :, None] == columns[None, None, :]).astype(jnp.float32)


def allsum(values):
    for axis in ("dev", "grp"):
        devices = lax.axis_size(axis)
        assert devices & (devices - 1) == 0
        step = 1
        while step < devices:
            pairs = [(i, i ^ step) for i in range(devices)]
            values = values + lax.ppermute(values, axis, pairs)
            step *= 2
    return values


def share_nodes(slab):
    for axis, dim in (("dev", 1), ("grp", 3)):
        devices, length = (lax.axis_size(axis), slab.shape[dim])
        up = [(i, i + 1) for i in range(devices - 1)]
        down = [(j, i) for i, j in up]
        last = lax.index_in_dim(slab, length - 1, axis=dim, keepdims=False)
        first = lax.index_in_dim(slab, 0, axis=dim, keepdims=False)
        before = lax.ppermute(last, axis, up)
        after = lax.ppermute(first, axis, down)
        head = lax.index_in_dim(slab, 0, axis=dim) + jnp.expand_dims(before, dim)
        tail = lax.index_in_dim(slab, length - 1, axis=dim) + jnp.expand_dims(after, dim)
        middle = lax.slice_in_dim(slab, 1, length - 1, axis=dim)
        slab = jnp.concatenate([head, middle, tail], axis=dim)
    return slab


def assemble(gathered):
    groups, bricks, comps, nbx, nby, nbz = gathered.shape
    highest = lax.Precision.HIGHEST
    place_x = scatter_matrix(bricks, nbx - 1)
    place_z = scatter_matrix(groups, nbz - 1)
    along_x = jnp.einsum("pqcijk,qix->pcxjk", gathered, place_x, precision=highest)
    return jnp.einsum("pcxjk,pkz->cxjz", along_x, place_z, precision=highest)


def local(ref_volume, def_volume, shifts, init_disp, precond):
    width_x, rows_y, depth_z = ref_volume.shape
    dev_count = lax.axis_size("dev")
    grp_count = lax.axis_size("grp")
    grp_index = lax.axis_index("grp")
    dev_index = lax.axis_index("dev")
    voxel_count = float(width_x * rows_y * depth_z * dev_count * grp_count)
    margin = SMAX + 1
    offset = shifts[0, 0]
    widened = with_halo(def_volume, (("dev", 0),), margin)
    framed = with_halo(widened, (("grp", 2),), 1)
    window = lax.dynamic_slice_in_dim(framed, offset + margin - 1, width_x + 2, 0)
    window = jnp.pad(window, ((0, 0), (1, 1), (0, 0))).astype(jnp.float32)
    slopes = gradients(window)
    sample = window[1:-1, 1:-1, 1:-1]
    target = ref_volume.astype(jnp.float32)
    elements_x = width_x // E
    elements_z = depth_z // E
    nodes_y = rows_y // E + 1
    hat_x = hat_matrix(width_x, elements_x + 1)
    hat_y = hat_matrix(rows_y, nodes_y)
    hat_z = hat_matrix(depth_z, elements_z + 1)
    corner = (0, dev_index * elements_x, 0, grp_index * elements_z)
    extent = (3, elements_x + 1, nodes_y, elements_z + 1)
    local_nodes = lax.dynamic_slice(init_disp, corner, extent)
    local_precond = lax.dynamic_slice(precond, corner, extent)
    target_sums = jnp.stack([jnp.sum(target), jnp.sum(target * target)])
    residual = target
    total_slab = None
    mean_ref = var_ref = None
    for iteration in range(ITERS):
        shift_field = expand_x(interpolate(local_nodes, hat_y, hat_z), hat_x)
        warped = sample + jnp.sum(shift_field * slopes, axis=0)
        image_sums = jnp.stack([jnp.sum(warped), jnp.sum(warped * warped)])
        if iteration == 0:
            sums = allsum(jnp.concatenate([target_sums, image_sums]))
            mean_ref = sums[0] / voxel_count
            var_ref = sums[1] / voxel_count - mean_ref * mean_ref
            image_sums = sums[2:]
        else:
            image_sums = allsum(image_sums)
        mean_img = image_sums[0] / voxel_count
        var_img = image_sums[1] / voxel_count - mean_img * mean_img
        ratio = jnp.sqrt((var_ref + epsilon) / (var_img + epsilon))
        residual = target - mean_ref - ratio * (warped - mean_img)
        slab = restrict(slopes * residual[None], hat_x, hat_y, hat_z)
        total_slab = slab if total_slab is None else total_slab + slab
        if iteration + 1 < ITERS:
            local_nodes = local_nodes + local_precond * share_nodes(slab)
    squares = jnp.sum(residual * residual)
    packed = jnp.concatenate([total_slab.reshape(-1), squares[None]])
    gathered = lax.all_gather(packed.reshape(2, -1), ("grp", "dev")).reshape(grp_count * dev_count, -1)
    pieces = gathered[:, :-1].reshape((grp_count, dev_count) + total_slab.shape)
    forces = assemble(pieces)
    motion = init_disp + precond * forces
    misfit = jnp.sqrt(jnp.sum(gathered[:, -1]) / voxel_count)
    return (motion, residual, misfit)


def solution(mesh):
    placed = (P("dev", None, "grp"), P("dev", None, "grp"), P("grp", "dev"), P(), P())
    return jax.shard_map(
        local,
        mesh=mesh,
        in_specs=placed,
        out_specs=(P(), P("dev", None, "grp"), P()),
        check_vma=False,
    )
```

```python
import jax
import jax.numpy as jnp
from jax import lax
from jax.sharding import PartitionSpec as P

E = 16
SMAX = 8
ITERS = 2


epsilon = 1e-06


def with_halo(shard, sides, width):
    for axis, dim in sides:
        devices, length = (lax.axis_size(axis), shard.shape[dim])
        up = [(i, (i + 1) % devices) for i in range(devices - 1)]
        down = [(j, i) for i, j in up]
        last = lax.slice_in_dim(shard, length - width, length, axis=dim)
        initial = lax.slice_in_dim(shard, 0, width, axis=dim)
        before = lax.ppermute(last, axis, up)
        after = lax.ppermute(initial, axis, down)
        shard = jnp.concatenate([before, shard, after], axis=dim)
    return shard


def hat_matrix(voxels, nodes):
    positions = jnp.arange(voxels, dtype=jnp.int32)
    element = positions // E
    fraction = (positions - element * E).astype(jnp.float32) / E
    columns = jnp.arange(nodes, dtype=jnp.int32)
    left_part = (columns[None, :] == element[:, None]).astype(jnp.float32) * (1.0 - fraction)[
        :, None
    ]
    right_part = (columns[None, :] == element[:, None] + 1).astype(jnp.float32) * fraction[:, None]
    return left_part + right_part


def smooth(values, direction):
    extent = values.shape[direction]
    lower = lax.slice_in_dim(values, 0, extent - 2, axis=direction)
    middle = lax.slice_in_dim(values, 1, extent - 1, axis=direction)
    upper = lax.slice_in_dim(values, 2, extent, axis=direction)
    return (lower + 4.0 * middle + upper) / 6.0


def differ(values, direction):
    extent = values.shape[direction]
    lower = lax.slice_in_dim(values, 0, extent - 2, axis=direction)
    upper = lax.slice_in_dim(values, 2, extent, axis=direction)
    return 0.5 * (upper - lower)


def gradients(window):
    smooth_z = smooth(window, 2)
    slope_x = differ(smooth(smooth_z, 1), 0)
    slope_y = smooth(differ(smooth_z, 1), 0)
    slope_z = smooth(smooth(differ(window, 2), 1), 0)
    return (slope_x, slope_y, slope_z)


def interpolate(local_nodes, hat_y, hat_z):
    highest = lax.Precision.HIGHEST
    partial_z = jnp.einsum("cijk,zk->cijz", local_nodes, hat_z, precision=highest)
    return jnp.einsum("cijz,yj->ciyz", partial_z, hat_y, precision=highest)


def expand_x(partial_y, hat_x):
    return sum(
        hat_x[None, :, i, None, None] * partial_y[:, i, None] for i in range(hat_x.shape[1])
    )


def restrict(terms, hat_x, hat_y, hat_z):
    highest = lax.Precision.HIGHEST
    partial_x = jnp.stack(
        [jnp.sum(terms * hat_x[None, :, i, None, None], axis=1) for i in range(hat_x.shape[1])],
        axis=1,
    )
    partial_y = jnp.einsum("ciyz,yj->cijz", partial_x, hat_y, precision=highest)
    return jnp.einsum("cijz,zk->cijk", partial_y, hat_z, precision=highest)


def scatter_matrix(bricks, elements):
    columns = jnp.arange(bricks * elements + 1, dtype=jnp.int32)
    starts = jnp.arange(bricks, dtype=jnp.int32)[:, None] * elements
    rows = starts + jnp.arange(elements + 1, dtype=jnp.int32)[None, :]
    return (rows[:, :, None] == columns[None, None, :]).astype(jnp.float32)


def allsum(values):
    for axis in ("dev", "grp"):
        devices = lax.axis_size(axis)
        assert devices & (devices - 1) == 0
        step = 1
        while step < devices:
            pairs = [(i, i ^ step) for i in range(devices)]
            values = values + lax.ppermute(values, axis, pairs)
            step *= 2
    return values


def share_nodes(slab):
    for axis, dim in (("dev", 1), ("grp", 3)):
        devices, length = (lax.axis_size(axis), slab.shape[dim])
        up = [(i, i + 1) for i in range(devices - 1)]
        down = [(j, i) for i, j in up]
        last = lax.index_in_dim(slab, length - 1, axis=dim, keepdims=False)
        first = lax.index_in_dim(slab, 0, axis=dim, keepdims=False)
        before = lax.ppermute(last, axis, up)
        after = lax.ppermute(first, axis, down)
        head = lax.index_in_dim(slab, 0, axis=dim) + jnp.expand_dims(before, dim)
        tail = lax.index_in_dim(slab, length - 1, axis=dim) + jnp.expand_dims(after, dim)
        middle = lax.slice_in_dim(slab, 1, length - 1, axis=dim)
        slab = jnp.concatenate([head, middle, tail], axis=dim)
    return slab


def assemble(gathered):
    groups, bricks, comps, nbx, nby, nbz = gathered.shape
    highest = lax.Precision.HIGHEST
    place_x = scatter_matrix(bricks, nbx - 1)
    place_z = scatter_matrix(groups, nbz - 1)
    along_x = jnp.einsum("pqcijk,qix->pcxjk", gathered, place_x, precision=highest)
    return jnp.einsum("pcxjk,pkz->cxjz", along_x, place_z, precision=highest)


def local(ref_volume, def_volume, shifts, init_disp, precond):
    width_x, rows_y, depth_z = ref_volume.shape
    dev_count = lax.axis_size("dev")
    grp_count = lax.axis_size("grp")
    grp_index = lax.axis_index("grp")
    dev_index = lax.axis_index("dev")
    voxel_count = float(width_x * rows_y * depth_z * dev_count * grp_count)
    margin = SMAX + 1
    offset = shifts[0, 0]
    widened = with_halo(def_volume, (("dev", 0),), margin)
    framed = with_halo(widened, (("grp", 2),), 1)
    window = lax.dynamic_slice_in_dim(framed, offset + margin - 1, width_x + 2, 0)
    window = jnp.pad(window, ((0, 0), (1, 1), (0, 0))).astype(jnp.float32)
    slopes = gradients(window)
    sample = window[1:-1, 1:-1, 1:-1]
    target = ref_volume.astype(jnp.float32)
    elements_x = width_x // E
    elements_z = depth_z // E
    nodes_y = rows_y // E + 1
    hat_x = hat_matrix(width_x, elements_x + 1)
    hat_y = hat_matrix(rows_y, nodes_y)
    hat_z = hat_matrix(depth_z, elements_z + 1)
    corner = (0, dev_index * elements_x, 0, grp_index * elements_z)
    extent = (3, elements_x + 1, nodes_y, elements_z + 1)
    local_nodes = lax.dynamic_slice(init_disp, corner, extent)
    local_precond = lax.dynamic_slice(precond, corner, extent)
    target_sums = jnp.stack([jnp.sum(target), jnp.sum(target * target)])
    fixed_a = restrict(jnp.stack([s * target for s in slopes]), hat_x, hat_y, hat_z)
    fixed_b = restrict(jnp.stack(slopes), hat_x, hat_y, hat_z)
    residual = target
    total_slab = None
    mean_ref = var_ref = None
    for iteration in range(ITERS):
        shift_field = expand_x(interpolate(local_nodes, hat_y, hat_z), hat_x)
        warped = sample + sum(shift_field[c] * slopes[c] for c in range(3))
        image_sums = jnp.stack([jnp.sum(warped), jnp.sum(warped * warped)])
        moving = restrict(jnp.stack([s * warped for s in slopes]), hat_x, hat_y, hat_z)
        if iteration == 0:
            sums = allsum(jnp.concatenate([target_sums, image_sums]))
            mean_ref = sums[0] / voxel_count
            var_ref = sums[1] / voxel_count - mean_ref * mean_ref
            image_sums = sums[2:]
        else:
            image_sums = allsum(image_sums)
        mean_img = image_sums[0] / voxel_count
        var_img = image_sums[1] / voxel_count - mean_img * mean_img
        ratio = jnp.sqrt((var_ref + epsilon) / (var_img + epsilon))
        slab = fixed_a - mean_ref * fixed_b - ratio * (moving - mean_img * fixed_b)
        total_slab = slab if total_slab is None else total_slab + slab
        if iteration + 1 < ITERS:
            local_nodes = local_nodes + local_precond * share_nodes(slab)
        else:
            residual = target - mean_ref - ratio * (warped - mean_img)
    squares = jnp.sum(residual * residual)
    packed = jnp.concatenate([total_slab.reshape(-1), squares[None]])
    gathered = lax.all_gather(packed.reshape(2, -1), ("grp", "dev")).reshape(grp_count * dev_count, -1)
    pieces = gathered[:, :-1].reshape((grp_count, dev_count) + total_slab.shape)
    forces = assemble(pieces)
    motion = init_disp + precond * forces
    misfit = jnp.sqrt(jnp.sum(gathered[:, -1]) / voxel_count)
    return (motion, residual, misfit)


def solution(mesh):
    placed = (P("dev", None, "grp"), P("dev", None, "grp"), P("grp", "dev"), P(), P())
    return jax.shard_map(
        local,
        mesh=mesh,
        in_specs=placed,
        out_specs=(P(), P("dev", None, "grp"), P()),
        check_vma=False,
    )
```

```python
import jax
import jax.numpy as jnp
from jax import lax
from jax.sharding import PartitionSpec as P
from jax.experimental import pallas as pl
from jax.experimental.pallas import tpu as pltpu

E = 16
SMAX = 8
ITERS = 2


epsilon = 1e-06


def with_halo(shard, sides, width):
    for axis, dim in sides:
        devices, length = (lax.axis_size(axis), shard.shape[dim])
        up = [(i, (i + 1) % devices) for i in range(devices - 1)]
        down = [(j, i) for i, j in up]
        last = lax.slice_in_dim(shard, length - width, length, axis=dim)
        initial = lax.slice_in_dim(shard, 0, width, axis=dim)
        before = lax.ppermute(last, axis, up)
        after = lax.ppermute(initial, axis, down)
        shard = jnp.concatenate([before, shard, after], axis=dim)
    return shard


from jax.experimental import pallas as pl
from jax.experimental.pallas import tpu as pltpu

PLANES = 16

def _slope_kernel(w_ref, sl_ref, sm_ref):
    step = pl.program_id(0)
    _, wx, wy = w_ref.shape
    bx = wx - 2
    lane = lax.broadcasted_iota(jnp.int32, (wx, wy), 1)

    def lower(v):
        return jnp.where(lane == 0, 0.0, pltpu.roll(v, 1, 1))

    def upper(v):
        return jnp.where(lane == wy - 1, 0.0, pltpu.roll(v, wy - 1, 1))

    def body(k, carry):
        z = step * PLANES + k
        w0 = w_ref[z]
        w1 = w_ref[z + 1]
        w2 = w_ref[z + 2]
        a = (w0 + 4.0 * w1 + w2) / 6.0
        b = 0.5 * (w2 - w0)
        a_lo, a_hi = lower(a), upper(a)
        sya = (a_lo + 4.0 * a + a_hi) / 6.0
        dya = 0.5 * (a_hi - a_lo)
        b_lo, b_hi = lower(b), upper(b)
        syb = (b_lo + 4.0 * b + b_hi) / 6.0
        sl_ref[0, k] = 0.5 * (sya[2:] - sya[:bx])
        sl_ref[1, k] = (dya[:bx] + 4.0 * dya[1 : bx + 1] + dya[2:]) / 6.0
        sl_ref[2, k] = (syb[:bx] + 4.0 * syb[1 : bx + 1] + syb[2:]) / 6.0
        sm_ref[k] = w1[1 : bx + 1]
        return carry

    lax.fori_loop(0, PLANES, body, 0)


def slopes_zxy(w, interpret=False):
    wz, wx, wy = w.shape
    nz, bx = wz - 2, wx - 2
    assert nz % PLANES == 0
    return pl.pallas_call(
        _slope_kernel,
        grid=(nz // PLANES,),
        in_specs=[pl.BlockSpec((wz, wx, wy), lambda i: (0, 0, 0))],
        out_specs=[
            pl.BlockSpec((3, PLANES, bx, wy), lambda i: (0, i, 0, 0)),
            pl.BlockSpec((PLANES, bx, wy), lambda i: (i, 0, 0)),
        ],
        out_shape=[
            jax.ShapeDtypeStruct((3, nz, bx, wy), jnp.float32),
            jax.ShapeDtypeStruct((nz, bx, wy), jnp.float32),
        ],
        interpret=interpret,
    )(w)


def hat_matrix(voxels, nodes):
    positions = jnp.arange(voxels, dtype=jnp.int32)
    element = positions // E
    fraction = (positions - element * E).astype(jnp.float32) / E
    columns = jnp.arange(nodes, dtype=jnp.int32)
    left_part = (columns[None, :] == element[:, None]).astype(jnp.float32) * (1.0 - fraction)[
        :, None
    ]
    right_part = (columns[None, :] == element[:, None] + 1).astype(jnp.float32) * fraction[:, None]
    return left_part + right_part


def smooth(values, direction):
    extent = values.shape[direction]
    lower = lax.slice_in_dim(values, 0, extent - 2, axis=direction)
    middle = lax.slice_in_dim(values, 1, extent - 1, axis=direction)
    upper = lax.slice_in_dim(values, 2, extent, axis=direction)
    return (lower + 4.0 * middle + upper) / 6.0


def differ(values, direction):
    extent = values.shape[direction]
    lower = lax.slice_in_dim(values, 0, extent - 2, axis=direction)
    upper = lax.slice_in_dim(values, 2, extent, axis=direction)
    return 0.5 * (upper - lower)


def gradients(window):
    smooth_z = smooth(window, 2)
    slope_x = differ(smooth(smooth_z, 1), 0)
    slope_y = smooth(differ(smooth_z, 1), 0)
    slope_z = smooth(smooth(differ(window, 2), 1), 0)
    return jnp.stack([slope_x, slope_y, slope_z])


def interpolate(local_nodes, hat_y, hat_z):
    highest = lax.Precision.HIGHEST
    partial_z = jnp.einsum("cijk,zk->cijz", local_nodes, hat_z, precision=highest)
    return jnp.einsum("cijz,yj->ciyz", partial_z, hat_y, precision=highest)


def expand_x(partial_y, hat_x):
    return sum(
        hat_x[None, :, i, None, None] * partial_y[:, i, None] for i in range(hat_x.shape[1])
    )


def restrict(terms, hat_x, hat_y, hat_z):
    highest = lax.Precision.HIGHEST
    partial_x = jnp.stack(
        [jnp.sum(terms * hat_x[None, :, i, None, None], axis=1) for i in range(hat_x.shape[1])],
        axis=1,
    )
    partial_y = jnp.einsum("ciyz,yj->cijz", partial_x, hat_y, precision=highest)
    return jnp.einsum("cijz,zk->cijk", partial_y, hat_z, precision=highest)


def scatter_matrix(bricks, elements):
    columns = jnp.arange(bricks * elements + 1, dtype=jnp.int32)
    starts = jnp.arange(bricks, dtype=jnp.int32)[:, None] * elements
    rows = starts + jnp.arange(elements + 1, dtype=jnp.int32)[None, :]
    return (rows[:, :, None] == columns[None, None, :]).astype(jnp.float32)


def allsum(values):
    for axis in ("dev", "grp"):
        devices = lax.axis_size(axis)
        assert devices & (devices - 1) == 0
        step = 1
        while step < devices:
            pairs = [(i, i ^ step) for i in range(devices)]
            values = values + lax.ppermute(values, axis, pairs)
            step *= 2
    return values


def share_nodes(slab):
    for axis, dim in (("dev", 1), ("grp", 3)):
        devices, length = (lax.axis_size(axis), slab.shape[dim])
        up = [(i, i + 1) for i in range(devices - 1)]
        down = [(j, i) for i, j in up]
        last = lax.index_in_dim(slab, length - 1, axis=dim, keepdims=False)
        first = lax.index_in_dim(slab, 0, axis=dim, keepdims=False)
        before = lax.ppermute(last, axis, up)
        after = lax.ppermute(first, axis, down)
        head = lax.index_in_dim(slab, 0, axis=dim) + jnp.expand_dims(before, dim)
        tail = lax.index_in_dim(slab, length - 1, axis=dim) + jnp.expand_dims(after, dim)
        middle = lax.slice_in_dim(slab, 1, length - 1, axis=dim)
        slab = jnp.concatenate([head, middle, tail], axis=dim)
    return slab


def assemble(gathered):
    groups, bricks, comps, nbx, nby, nbz = gathered.shape
    highest = lax.Precision.HIGHEST
    place_x = scatter_matrix(bricks, nbx - 1)
    place_z = scatter_matrix(groups, nbz - 1)
    along_x = jnp.einsum("pqcijk,qix->pcxjk", gathered, place_x, precision=highest)
    return jnp.einsum("pcxjk,pkz->cxjz", along_x, place_z, precision=highest)


def local(ref_volume, def_volume, shifts, init_disp, precond):
    width_x, rows_y, depth_z = ref_volume.shape
    dev_count = lax.axis_size("dev")
    grp_count = lax.axis_size("grp")
    grp_index = lax.axis_index("grp")
    dev_index = lax.axis_index("dev")
    voxel_count = float(width_x * rows_y * depth_z * dev_count * grp_count)
    margin = SMAX + 1
    offset = shifts[0, 0]
    widened = with_halo(def_volume, (("dev", 0),), margin)
    framed = with_halo(widened, (("grp", 2),), 1)
    window = lax.dynamic_slice_in_dim(framed, offset + margin - 1, width_x + 2, 0)
    window = jnp.transpose(window.astype(jnp.float32), (2, 0, 1))
    slopes, sample = slopes_zxy(window)
    slopes = jnp.transpose(slopes, (0, 2, 3, 1))
    sample = jnp.transpose(sample, (1, 2, 0))
    target = ref_volume.astype(jnp.float32)
    elements_x = width_x // E
    elements_z = depth_z // E
    nodes_y = rows_y // E + 1
    hat_x = hat_matrix(width_x, elements_x + 1)
    hat_y = hat_matrix(rows_y, nodes_y)
    hat_z = hat_matrix(depth_z, elements_z + 1)
    corner = (0, dev_index * elements_x, 0, grp_index * elements_z)
    extent = (3, elements_x + 1, nodes_y, elements_z + 1)
    local_nodes = lax.dynamic_slice(init_disp, corner, extent)
    local_precond = lax.dynamic_slice(precond, corner, extent)
    target_sums = jnp.stack([jnp.sum(target), jnp.sum(target * target)])
    residual = target
    total_slab = None
    mean_ref = var_ref = None
    for iteration in range(ITERS):
        shift_field = expand_x(interpolate(local_nodes, hat_y, hat_z), hat_x)
        warped = sample + jnp.sum(shift_field * slopes, axis=0)
        image_sums = jnp.stack([jnp.sum(warped), jnp.sum(warped * warped)])
        if iteration == 0:
            sums = allsum(jnp.concatenate([target_sums, image_sums]))
            mean_ref = sums[0] / voxel_count
            var_ref = sums[1] / voxel_count - mean_ref * mean_ref
            image_sums = sums[2:]
        else:
            image_sums = allsum(image_sums)
        mean_img = image_sums[0] / voxel_count
        var_img = image_sums[1] / voxel_count - mean_img * mean_img
        ratio = jnp.sqrt((var_ref + epsilon) / (var_img + epsilon))
        residual = target - mean_ref - ratio * (warped - mean_img)
        slab = restrict(slopes * residual[None], hat_x, hat_y, hat_z)
        total_slab = slab if total_slab is None else total_slab + slab
        if iteration + 1 < ITERS:
            local_nodes = local_nodes + local_precond * share_nodes(slab)
    squares = jnp.sum(residual * residual)
    packed = jnp.concatenate([total_slab.reshape(-1), squares[None]])
    gathered = lax.all_gather(packed.reshape(2, -1), ("grp", "dev")).reshape(grp_count * dev_count, -1)
    pieces = gathered[:, :-1].reshape((grp_count, dev_count) + total_slab.shape)
    forces = assemble(pieces)
    motion = init_disp + precond * forces
    misfit = jnp.sqrt(jnp.sum(gathered[:, -1]) / voxel_count)
    return (motion, residual, misfit)


def solution(mesh):
    placed = (P("dev", None, "grp"), P("dev", None, "grp"), P("grp", "dev"), P(), P())
    return jax.shard_map(
        local,
        mesh=mesh,
        in_specs=placed,
        out_specs=(P(), P("dev", None, "grp"), P()),
        check_vma=False,
    )
```

```python
import jax
import jax.numpy as jnp
from jax import lax
from jax.sharding import PartitionSpec as P
from jax.experimental import pallas as pl
from jax.experimental.pallas import tpu as pltpu

E = 16
SMAX = 8
ITERS = 2


epsilon = 1e-06


def with_halo(shard, sides, width):
    for axis, dim in sides:
        devices, length = (lax.axis_size(axis), shard.shape[dim])
        up = [(i, (i + 1) % devices) for i in range(devices - 1)]
        down = [(j, i) for i, j in up]
        last = lax.slice_in_dim(shard, length - width, length, axis=dim)
        initial = lax.slice_in_dim(shard, 0, width, axis=dim)
        before = lax.ppermute(last, axis, up)
        after = lax.ppermute(initial, axis, down)
        shard = jnp.concatenate([before, shard, after], axis=dim)
    return shard


from jax.experimental import pallas as pl
from jax.experimental.pallas import tpu as pltpu

PLANES = 16

def _slope_kernel(w_ref, sl_ref, sm_ref):
    step = pl.program_id(0)
    _, wx, wy = w_ref.shape
    bx = wx - 2
    lane = lax.broadcasted_iota(jnp.int32, (wx, wy), 1)

    def lower(v):
        return jnp.where(lane == 0, 0.0, pltpu.roll(v, 1, 1))

    def upper(v):
        return jnp.where(lane == wy - 1, 0.0, pltpu.roll(v, wy - 1, 1))

    def body(k, carry):
        z = step * PLANES + k
        w0 = w_ref[z].astype(jnp.float32)
        w1 = w_ref[z + 1].astype(jnp.float32)
        w2 = w_ref[z + 2].astype(jnp.float32)
        sixth = 1.0 / 6.0
        a = (w0 + 4.0 * w1 + w2) * sixth
        b = 0.5 * (w2 - w0)
        a_lo, a_hi = lower(a), upper(a)
        sya = (a_lo + 4.0 * a + a_hi) * sixth
        dya = 0.5 * (a_hi - a_lo)
        b_lo, b_hi = lower(b), upper(b)
        syb = (b_lo + 4.0 * b + b_hi) * sixth
        sl_ref[0, k] = 0.5 * (sya[2:] - sya[:bx])
        sl_ref[1, k] = (dya[:bx] + 4.0 * dya[1 : bx + 1] + dya[2:]) * sixth
        sl_ref[2, k] = (syb[:bx] + 4.0 * syb[1 : bx + 1] + syb[2:]) * sixth
        sm_ref[k] = w1[1 : bx + 1]
        return carry

    lax.fori_loop(0, PLANES, body, 0)


def slopes_zxy(w, interpret=False):
    wz, wx, wy = w.shape
    nz, bx = wz - 2, wx - 2
    assert nz % PLANES == 0
    return pl.pallas_call(
        _slope_kernel,
        grid=(nz // PLANES,),
        in_specs=[pl.BlockSpec((wz, wx, wy), lambda i: (0, 0, 0))],
        out_specs=[
            pl.BlockSpec((3, PLANES, bx, wy), lambda i: (0, i, 0, 0)),
            pl.BlockSpec((PLANES, bx, wy), lambda i: (i, 0, 0)),
        ],
        out_shape=[
            jax.ShapeDtypeStruct((3, nz, bx, wy), jnp.float32),
            jax.ShapeDtypeStruct((nz, bx, wy), jnp.float32),
        ],
        interpret=interpret,
    )(w)


def hat_matrix(voxels, nodes):
    positions = jnp.arange(voxels, dtype=jnp.int32)
    element = positions // E
    fraction = (positions - element * E).astype(jnp.float32) / E
    columns = jnp.arange(nodes, dtype=jnp.int32)
    left_part = (columns[None, :] == element[:, None]).astype(jnp.float32) * (1.0 - fraction)[
        :, None
    ]
    right_part = (columns[None, :] == element[:, None] + 1).astype(jnp.float32) * fraction[:, None]
    return left_part + right_part


def smooth(values, direction):
    extent = values.shape[direction]
    lower = lax.slice_in_dim(values, 0, extent - 2, axis=direction)
    middle = lax.slice_in_dim(values, 1, extent - 1, axis=direction)
    upper = lax.slice_in_dim(values, 2, extent, axis=direction)
    return (lower + 4.0 * middle + upper) / 6.0


def differ(values, direction):
    extent = values.shape[direction]
    lower = lax.slice_in_dim(values, 0, extent - 2, axis=direction)
    upper = lax.slice_in_dim(values, 2, extent, axis=direction)
    return 0.5 * (upper - lower)


def gradients(window):
    smooth_z = smooth(window, 2)
    slope_x = differ(smooth(smooth_z, 1), 0)
    slope_y = smooth(differ(smooth_z, 1), 0)
    slope_z = smooth(smooth(differ(window, 2), 1), 0)
    return jnp.stack([slope_x, slope_y, slope_z])


def interpolate(local_nodes, hat_y, hat_z):
    highest = lax.Precision.HIGHEST
    partial_z = jnp.einsum("cijk,zk->cijz", local_nodes, hat_z, precision=highest)
    return jnp.einsum("cijz,yj->ciyz", partial_z, hat_y, precision=highest)


def expand_x(partial_y, hat_x):
    return sum(
        hat_x[None, :, i, None, None] * partial_y[:, i, None] for i in range(hat_x.shape[1])
    )


def restrict(terms, hat_x, hat_y, hat_z):
    highest = lax.Precision.HIGHEST
    partial_x = jnp.stack(
        [jnp.sum(terms * hat_x[None, :, i, None, None], axis=1) for i in range(hat_x.shape[1])],
        axis=1,
    )
    partial_y = jnp.einsum("ciyz,yj->cijz", partial_x, hat_y, precision=highest)
    return jnp.einsum("cijz,zk->cijk", partial_y, hat_z, precision=highest)


def scatter_matrix(bricks, elements):
    columns = jnp.arange(bricks * elements + 1, dtype=jnp.int32)
    starts = jnp.arange(bricks, dtype=jnp.int32)[:, None] * elements
    rows = starts + jnp.arange(elements + 1, dtype=jnp.int32)[None, :]
    return (rows[:, :, None] == columns[None, None, :]).astype(jnp.float32)


def allsum(values):
    for axis in ("dev", "grp"):
        devices = lax.axis_size(axis)
        assert devices & (devices - 1) == 0
        step = 1
        while step < devices:
            pairs = [(i, i ^ step) for i in range(devices)]
            values = values + lax.ppermute(values, axis, pairs)
            step *= 2
    return values


def share_nodes(slab):
    for axis, dim in (("dev", 1), ("grp", 3)):
        devices, length = (lax.axis_size(axis), slab.shape[dim])
        up = [(i, i + 1) for i in range(devices - 1)]
        down = [(j, i) for i, j in up]
        last = lax.index_in_dim(slab, length - 1, axis=dim, keepdims=False)
        first = lax.index_in_dim(slab, 0, axis=dim, keepdims=False)
        before = lax.ppermute(last, axis, up)
        after = lax.ppermute(first, axis, down)
        head = lax.index_in_dim(slab, 0, axis=dim) + jnp.expand_dims(before, dim)
        tail = lax.index_in_dim(slab, length - 1, axis=dim) + jnp.expand_dims(after, dim)
        middle = lax.slice_in_dim(slab, 1, length - 1, axis=dim)
        slab = jnp.concatenate([head, middle, tail], axis=dim)
    return slab


def assemble(gathered):
    groups, bricks, comps, nbx, nby, nbz = gathered.shape
    highest = lax.Precision.HIGHEST
    place_x = scatter_matrix(bricks, nbx - 1)
    place_z = scatter_matrix(groups, nbz - 1)
    along_x = jnp.einsum("pqcijk,qix->pcxjk", gathered, place_x, precision=highest)
    return jnp.einsum("pcxjk,pkz->cxjz", along_x, place_z, precision=highest)


def local(ref_volume, def_volume, shifts, init_disp, precond):
    width_x, rows_y, depth_z = ref_volume.shape
    dev_count = lax.axis_size("dev")
    grp_count = lax.axis_size("grp")
    grp_index = lax.axis_index("grp")
    dev_index = lax.axis_index("dev")
    voxel_count = float(width_x * rows_y * depth_z * dev_count * grp_count)
    margin = SMAX + 1
    offset = shifts[0, 0]
    widened = with_halo(def_volume, (("dev", 0),), margin)
    framed = with_halo(widened, (("grp", 2),), 1)
    window = lax.dynamic_slice_in_dim(framed, offset + margin - 1, width_x + 2, 0)
    window = jnp.transpose(window, (2, 0, 1))
    slopes, sample = slopes_zxy(window)
    slopes = jnp.transpose(slopes, (0, 2, 3, 1))
    sample = jnp.transpose(sample, (1, 2, 0))
    target = ref_volume.astype(jnp.float32)
    elements_x = width_x // E
    elements_z = depth_z // E
    nodes_y = rows_y // E + 1
    hat_x = hat_matrix(width_x, elements_x + 1)
    hat_y = hat_matrix(rows_y, nodes_y)
    hat_z = hat_matrix(depth_z, elements_z + 1)
    corner = (0, dev_index * elements_x, 0, grp_index * elements_z)
    extent = (3, elements_x + 1, nodes_y, elements_z + 1)
    local_nodes = lax.dynamic_slice(init_disp, corner, extent)
    local_precond = lax.dynamic_slice(precond, corner, extent)
    target_sums = jnp.stack([jnp.sum(target), jnp.sum(target * target)])
    residual = target
    total_slab = None
    mean_ref = var_ref = None
    for iteration in range(ITERS):
        shift_field = expand_x(interpolate(local_nodes, hat_y, hat_z), hat_x)
        warped = sample + jnp.sum(shift_field * slopes, axis=0)
        image_sums = jnp.stack([jnp.sum(warped), jnp.sum(warped * warped)])
        if iteration == 0:
            sums = allsum(jnp.concatenate([target_sums, image_sums]))
            mean_ref = sums[0] / voxel_count
            var_ref = sums[1] / voxel_count - mean_ref * mean_ref
            image_sums = sums[2:]
        else:
            image_sums = allsum(image_sums)
        mean_img = image_sums[0] / voxel_count
        var_img = image_sums[1] / voxel_count - mean_img * mean_img
        ratio = jnp.sqrt((var_ref + epsilon) / (var_img + epsilon))
        residual = target - mean_ref - ratio * (warped - mean_img)
        slab = restrict(slopes * residual[None], hat_x, hat_y, hat_z)
        total_slab = slab if total_slab is None else total_slab + slab
        if iteration + 1 < ITERS:
            local_nodes = local_nodes + local_precond * share_nodes(slab)
    squares = jnp.sum(residual * residual)
    packed = jnp.concatenate([total_slab.reshape(-1), squares[None]])
    gathered = lax.all_gather(packed.reshape(2, -1), ("grp", "dev")).reshape(grp_count * dev_count, -1)
    pieces = gathered[:, :-1].reshape((grp_count, dev_count) + total_slab.shape)
    forces = assemble(pieces)
    motion = init_disp + precond * forces
    misfit = jnp.sqrt(jnp.sum(gathered[:, -1]) / voxel_count)
    return (motion, residual, misfit)


def solution(mesh):
    placed = (P("dev", None, "grp"), P("dev", None, "grp"), P("grp", "dev"), P(), P())
    return jax.shard_map(
        local,
        mesh=mesh,
        in_specs=placed,
        out_specs=(P(), P("dev", None, "grp"), P()),
        check_vma=False,
    )
```

```python
import jax
import jax.numpy as jnp
from jax import lax
from jax.sharding import PartitionSpec as P
from jax.experimental import pallas as pl
from jax.experimental.pallas import tpu as pltpu

E = 16
SMAX = 8
ITERS = 2


epsilon = 1e-06


def with_halo(shard, sides, width):
    for axis, dim in sides:
        devices, length = (lax.axis_size(axis), shard.shape[dim])
        up = [(i, (i + 1) % devices) for i in range(devices - 1)]
        down = [(j, i) for i, j in up]
        last = lax.slice_in_dim(shard, length - width, length, axis=dim)
        initial = lax.slice_in_dim(shard, 0, width, axis=dim)
        before = lax.ppermute(last, axis, up)
        after = lax.ppermute(initial, axis, down)
        shard = jnp.concatenate([before, shard, after], axis=dim)
    return shard


from jax.experimental import pallas as pl
from jax.experimental.pallas import tpu as pltpu

PLANES = 16

def _slope_kernel(w_ref, sl_ref, sm_ref):
    step = pl.program_id(0)
    _, wx, wy = w_ref.shape
    bx = wx - 2
    lane = lax.broadcasted_iota(jnp.int32, (wx, wy), 1)

    def lower(v):
        return jnp.where(lane == 0, 0.0, pltpu.roll(v, 1, 1))

    def upper(v):
        return jnp.where(lane == wy - 1, 0.0, pltpu.roll(v, wy - 1, 1))

    def body(k, carry):
        z = step * PLANES + k
        w0 = w_ref[z].astype(jnp.float32)
        w1 = w_ref[z + 1].astype(jnp.float32)
        w2 = w_ref[z + 2].astype(jnp.float32)
        sixth = 1.0 / 6.0
        a = (w0 + 4.0 * w1 + w2) * sixth
        b = 0.5 * (w2 - w0)
        a_lo, a_hi = lower(a), upper(a)
        sya = (a_lo + 4.0 * a + a_hi) * sixth
        dya = 0.5 * (a_hi - a_lo)
        b_lo, b_hi = lower(b), upper(b)
        syb = (b_lo + 4.0 * b + b_hi) * sixth
        sl_ref[0, k] = 0.5 * (sya[2:] - sya[:bx])
        sl_ref[1, k] = (dya[:bx] + 4.0 * dya[1 : bx + 1] + dya[2:]) * sixth
        sl_ref[2, k] = (syb[:bx] + 4.0 * syb[1 : bx + 1] + syb[2:]) * sixth
        sm_ref[k] = w1[1 : bx + 1]
        return carry

    lax.fori_loop(0, PLANES, body, 0, unroll=True)


def slopes_zxy(w, interpret=False):
    wz, wx, wy = w.shape
    nz, bx = wz - 2, wx - 2
    assert nz % PLANES == 0
    return pl.pallas_call(
        _slope_kernel,
        grid=(nz // PLANES,),
        in_specs=[pl.BlockSpec((wz, wx, wy), lambda i: (0, 0, 0))],
        out_specs=[
            pl.BlockSpec((3, PLANES, bx, wy), lambda i: (0, i, 0, 0)),
            pl.BlockSpec((PLANES, bx, wy), lambda i: (i, 0, 0)),
        ],
        out_shape=[
            jax.ShapeDtypeStruct((3, nz, bx, wy), jnp.float32),
            jax.ShapeDtypeStruct((nz, bx, wy), jnp.float32),
        ],
        interpret=interpret,
    )(w)


def hat_matrix(voxels, nodes):
    positions = jnp.arange(voxels, dtype=jnp.int32)
    element = positions // E
    fraction = (positions - element * E).astype(jnp.float32) / E
    columns = jnp.arange(nodes, dtype=jnp.int32)
    left_part = (columns[None, :] == element[:, None]).astype(jnp.float32) * (1.0 - fraction)[
        :, None
    ]
    right_part = (columns[None, :] == element[:, None] + 1).astype(jnp.float32) * fraction[:, None]
    return left_part + right_part


def smooth(values, direction):
    extent = values.shape[direction]
    lower = lax.slice_in_dim(values, 0, extent - 2, axis=direction)
    middle = lax.slice_in_dim(values, 1, extent - 1, axis=direction)
    upper = lax.slice_in_dim(values, 2, extent, axis=direction)
    return (lower + 4.0 * middle + upper) / 6.0


def differ(values, direction):
    extent = values.shape[direction]
    lower = lax.slice_in_dim(values, 0, extent - 2, axis=direction)
    upper = lax.slice_in_dim(values, 2, extent, axis=direction)
    return 0.5 * (upper - lower)


def gradients(window):
    smooth_z = smooth(window, 2)
    slope_x = differ(smooth(smooth_z, 1), 0)
    slope_y = smooth(differ(smooth_z, 1), 0)
    slope_z = smooth(smooth(differ(window, 2), 1), 0)
    return jnp.stack([slope_x, slope_y, slope_z])


def interpolate(local_nodes, hat_y, hat_z):
    highest = lax.Precision.HIGHEST
    partial_z = jnp.einsum("cijk,zk->cijz", local_nodes, hat_z, precision=highest)
    return jnp.einsum("cijz,yj->ciyz", partial_z, hat_y, precision=highest)


def expand_x(partial_y, hat_x):
    return sum(
        hat_x[None, :, i, None, None] * partial_y[:, i, None] for i in range(hat_x.shape[1])
    )


def restrict(terms, hat_x, hat_y, hat_z):
    highest = lax.Precision.HIGHEST
    partial_x = jnp.stack(
        [jnp.sum(terms * hat_x[None, :, i, None, None], axis=1) for i in range(hat_x.shape[1])],
        axis=1,
    )
    partial_y = jnp.einsum("ciyz,yj->cijz", partial_x, hat_y, precision=highest)
    return jnp.einsum("cijz,zk->cijk", partial_y, hat_z, precision=highest)


def scatter_matrix(bricks, elements):
    columns = jnp.arange(bricks * elements + 1, dtype=jnp.int32)
    starts = jnp.arange(bricks, dtype=jnp.int32)[:, None] * elements
    rows = starts + jnp.arange(elements + 1, dtype=jnp.int32)[None, :]
    return (rows[:, :, None] == columns[None, None, :]).astype(jnp.float32)


def allsum(values):
    for axis in ("dev", "grp"):
        devices = lax.axis_size(axis)
        assert devices & (devices - 1) == 0
        step = 1
        while step < devices:
            pairs = [(i, i ^ step) for i in range(devices)]
            values = values + lax.ppermute(values, axis, pairs)
            step *= 2
    return values


def share_nodes(slab):
    for axis, dim in (("dev", 1), ("grp", 3)):
        devices, length = (lax.axis_size(axis), slab.shape[dim])
        up = [(i, i + 1) for i in range(devices - 1)]
        down = [(j, i) for i, j in up]
        last = lax.index_in_dim(slab, length - 1, axis=dim, keepdims=False)
        first = lax.index_in_dim(slab, 0, axis=dim, keepdims=False)
        before = lax.ppermute(last, axis, up)
        after = lax.ppermute(first, axis, down)
        head = lax.index_in_dim(slab, 0, axis=dim) + jnp.expand_dims(before, dim)
        tail = lax.index_in_dim(slab, length - 1, axis=dim) + jnp.expand_dims(after, dim)
        middle = lax.slice_in_dim(slab, 1, length - 1, axis=dim)
        slab = jnp.concatenate([head, middle, tail], axis=dim)
    return slab


def assemble(gathered):
    groups, bricks, comps, nbx, nby, nbz = gathered.shape
    highest = lax.Precision.HIGHEST
    place_x = scatter_matrix(bricks, nbx - 1)
    place_z = scatter_matrix(groups, nbz - 1)
    along_x = jnp.einsum("pqcijk,qix->pcxjk", gathered, place_x, precision=highest)
    return jnp.einsum("pcxjk,pkz->cxjz", along_x, place_z, precision=highest)


def local(ref_volume, def_volume, shifts, init_disp, precond):
    width_x, rows_y, depth_z = ref_volume.shape
    dev_count = lax.axis_size("dev")
    grp_count = lax.axis_size("grp")
    grp_index = lax.axis_index("grp")
    dev_index = lax.axis_index("dev")
    voxel_count = float(width_x * rows_y * depth_z * dev_count * grp_count)
    margin = SMAX + 1
    offset = shifts[0, 0]
    widened = with_halo(def_volume, (("dev", 0),), margin)
    framed = with_halo(widened, (("grp", 2),), 1)
    window = lax.dynamic_slice_in_dim(framed, offset + margin - 1, width_x + 2, 0)
    window = jnp.transpose(window, (2, 0, 1))
    slopes, sample = slopes_zxy(window)
    slopes = jnp.transpose(slopes, (0, 2, 3, 1))
    sample = jnp.transpose(sample, (1, 2, 0))
    target = ref_volume.astype(jnp.float32)
    elements_x = width_x // E
    elements_z = depth_z // E
    nodes_y = rows_y // E + 1
    hat_x = hat_matrix(width_x, elements_x + 1)
    hat_y = hat_matrix(rows_y, nodes_y)
    hat_z = hat_matrix(depth_z, elements_z + 1)
    corner = (0, dev_index * elements_x, 0, grp_index * elements_z)
    extent = (3, elements_x + 1, nodes_y, elements_z + 1)
    local_nodes = lax.dynamic_slice(init_disp, corner, extent)
    local_precond = lax.dynamic_slice(precond, corner, extent)
    target_sums = jnp.stack([jnp.sum(target), jnp.sum(target * target)])
    residual = target
    total_slab = None
    mean_ref = var_ref = None
    for iteration in range(ITERS):
        shift_field = expand_x(interpolate(local_nodes, hat_y, hat_z), hat_x)
        warped = sample + jnp.sum(shift_field * slopes, axis=0)
        image_sums = jnp.stack([jnp.sum(warped), jnp.sum(warped * warped)])
        if iteration == 0:
            sums = allsum(jnp.concatenate([target_sums, image_sums]))
            mean_ref = sums[0] / voxel_count
            var_ref = sums[1] / voxel_count - mean_ref * mean_ref
            image_sums = sums[2:]
        else:
            image_sums = allsum(image_sums)
        mean_img = image_sums[0] / voxel_count
        var_img = image_sums[1] / voxel_count - mean_img * mean_img
        ratio = jnp.sqrt((var_ref + epsilon) / (var_img + epsilon))
        residual = target - mean_ref - ratio * (warped - mean_img)
        slab = restrict(slopes * residual[None], hat_x, hat_y, hat_z)
        total_slab = slab if total_slab is None else total_slab + slab
        if iteration + 1 < ITERS:
            local_nodes = local_nodes + local_precond * share_nodes(slab)
    squares = jnp.sum(residual * residual)
    packed = jnp.concatenate([total_slab.reshape(-1), squares[None]])
    gathered = lax.all_gather(packed.reshape(2, -1), ("grp", "dev")).reshape(grp_count * dev_count, -1)
    pieces = gathered[:, :-1].reshape((grp_count, dev_count) + total_slab.shape)
    forces = assemble(pieces)
    motion = init_disp + precond * forces
    misfit = jnp.sqrt(jnp.sum(gathered[:, -1]) / voxel_count)
    return (motion, residual, misfit)


def solution(mesh):
    placed = (P("dev", None, "grp"), P("dev", None, "grp"), P("grp", "dev"), P(), P())
    return jax.shard_map(
        local,
        mesh=mesh,
        in_specs=placed,
        out_specs=(P(), P("dev", None, "grp"), P()),
        check_vma=False,
    )
```

```python
import jax
import jax.numpy as jnp
from jax import lax
from jax.sharding import PartitionSpec as P
from jax.experimental import pallas as pl
from jax.experimental.pallas import tpu as pltpu

E = 16
SMAX = 8
ITERS = 2


epsilon = 1e-06


def with_halo(shard, sides, width):
    for axis, dim in sides:
        devices, length = (lax.axis_size(axis), shard.shape[dim])
        up = [(i, (i + 1) % devices) for i in range(devices - 1)]
        down = [(j, i) for i, j in up]
        last = lax.slice_in_dim(shard, length - width, length, axis=dim)
        initial = lax.slice_in_dim(shard, 0, width, axis=dim)
        before = lax.ppermute(last, axis, up)
        after = lax.ppermute(initial, axis, down)
        shard = jnp.concatenate([before, shard, after], axis=dim)
    return shard


from jax.experimental import pallas as pl
from jax.experimental.pallas import tpu as pltpu

PLANES = 8


def _native_kernel(offset_ref, w_ref, lo_ref, hi_ref, sl_ref, sm_ref):
    step = pl.program_id(0)
    _, wy, wz = w_ref.shape
    row = lax.broadcasted_iota(jnp.int32, (wy, wz), 0)
    lane = lax.broadcasted_iota(jnp.int32, (wy, wz), 1)
    sixth = 1.0 / 6.0
    base = offset_ref[0] + SMAX + step * PLANES

    def planes(t):
        p = base + t
        w = w_ref[p].astype(jnp.float32)
        below = jnp.where(lane == 0, lo_ref[p].astype(jnp.float32), pltpu.roll(w, 1, 1))
        above = jnp.where(lane == wz - 1, hi_ref[p].astype(jnp.float32), pltpu.roll(w, wz - 1, 1))
        smooth_z = (below + 4.0 * w + above) * sixth
        differ_z = 0.5 * (above - below)
        s_lo = jnp.where(row == 0, 0.0, pltpu.roll(smooth_z, 1, 0))
        s_hi = jnp.where(row == wy - 1, 0.0, pltpu.roll(smooth_z, wy - 1, 0))
        d_lo = jnp.where(row == 0, 0.0, pltpu.roll(differ_z, 1, 0))
        d_hi = jnp.where(row == wy - 1, 0.0, pltpu.roll(differ_z, wy - 1, 0))
        return (
            (s_lo + 4.0 * smooth_z + s_hi) * sixth,
            0.5 * (s_hi - s_lo),
            (d_lo + 4.0 * differ_z + d_hi) * sixth,
            w,
        )

    window = [planes(0), planes(1)]
    for k in range(PLANES):
        window.append(planes(k + 2))
        prev, mid, nxt = window[k], window[k + 1], window[k + 2]
        sl_ref[0, k] = 0.5 * (nxt[0] - prev[0])
        sl_ref[1, k] = (prev[1] + 4.0 * mid[1] + nxt[1]) * sixth
        sl_ref[2, k] = (prev[2] + 4.0 * mid[2] + nxt[2]) * sixth
        sm_ref[k] = mid[3]


def native_slopes(offset, widened, below, above, width_x, interpret=False):
    _, wy, wz = widened.shape
    assert width_x % PLANES == 0
    whole = pl.BlockSpec(widened.shape, lambda i, o: (0, 0, 0))
    face = pl.BlockSpec(below.shape, lambda i, o: (0, 0, 0))
    spec = pltpu.PrefetchScalarGridSpec(
        num_scalar_prefetch=1,
        grid=(width_x // PLANES,),
        in_specs=[whole, face, face],
        out_specs=[
            pl.BlockSpec((3, PLANES, wy, wz), lambda i, o: (0, i, 0, 0)),
            pl.BlockSpec((PLANES, wy, wz), lambda i, o: (i, 0, 0)),
        ],
    )
    return pl.pallas_call(
        _native_kernel,
        grid_spec=spec,
        out_shape=[
            jax.ShapeDtypeStruct((3, width_x, wy, wz), jnp.float32),
            jax.ShapeDtypeStruct((width_x, wy, wz), jnp.float32),
        ],
        interpret=interpret,
    )(offset, widened, below, above)


def hat_matrix(voxels, nodes):
    positions = jnp.arange(voxels, dtype=jnp.int32)
    element = positions // E
    fraction = (positions - element * E).astype(jnp.float32) / E
    columns = jnp.arange(nodes, dtype=jnp.int32)
    left_part = (columns[None, :] == element[:, None]).astype(jnp.float32) * (1.0 - fraction)[
        :, None
    ]
    right_part = (columns[None, :] == element[:, None] + 1).astype(jnp.float32) * fraction[:, None]
    return left_part + right_part


def smooth(values, direction):
    extent = values.shape[direction]
    lower = lax.slice_in_dim(values, 0, extent - 2, axis=direction)
    middle = lax.slice_in_dim(values, 1, extent - 1, axis=direction)
    upper = lax.slice_in_dim(values, 2, extent, axis=direction)
    return (lower + 4.0 * middle + upper) / 6.0


def differ(values, direction):
    extent = values.shape[direction]
    lower = lax.slice_in_dim(values, 0, extent - 2, axis=direction)
    upper = lax.slice_in_dim(values, 2, extent, axis=direction)
    return 0.5 * (upper - lower)


def gradients(window):
    smooth_z = smooth(window, 2)
    slope_x = differ(smooth(smooth_z, 1), 0)
    slope_y = smooth(differ(smooth_z, 1), 0)
    slope_z = smooth(smooth(differ(window, 2), 1), 0)
    return jnp.stack([slope_x, slope_y, slope_z])


def interpolate(local_nodes, hat_y, hat_z):
    highest = lax.Precision.HIGHEST
    partial_z = jnp.einsum("cijk,zk->cijz", local_nodes, hat_z, precision=highest)
    return jnp.einsum("cijz,yj->ciyz", partial_z, hat_y, precision=highest)


def expand_x(partial_y, hat_x):
    return sum(
        hat_x[None, :, i, None, None] * partial_y[:, i, None] for i in range(hat_x.shape[1])
    )


def restrict(terms, hat_x, hat_y, hat_z):
    highest = lax.Precision.HIGHEST
    partial_x = jnp.stack(
        [jnp.sum(terms * hat_x[None, :, i, None, None], axis=1) for i in range(hat_x.shape[1])],
        axis=1,
    )
    partial_y = jnp.einsum("ciyz,yj->cijz", partial_x, hat_y, precision=highest)
    return jnp.einsum("cijz,zk->cijk", partial_y, hat_z, precision=highest)


def scatter_matrix(bricks, elements):
    columns = jnp.arange(bricks * elements + 1, dtype=jnp.int32)
    starts = jnp.arange(bricks, dtype=jnp.int32)[:, None] * elements
    rows = starts + jnp.arange(elements + 1, dtype=jnp.int32)[None, :]
    return (rows[:, :, None] == columns[None, None, :]).astype(jnp.float32)


def allsum(values):
    for axis in ("dev", "grp"):
        devices = lax.axis_size(axis)
        assert devices & (devices - 1) == 0
        step = 1
        while step < devices:
            pairs = [(i, i ^ step) for i in range(devices)]
            values = values + lax.ppermute(values, axis, pairs)
            step *= 2
    return values


def share_nodes(slab):
    for axis, dim in (("dev", 1), ("grp", 3)):
        devices, length = (lax.axis_size(axis), slab.shape[dim])
        up = [(i, i + 1) for i in range(devices - 1)]
        down = [(j, i) for i, j in up]
        last = lax.index_in_dim(slab, length - 1, axis=dim, keepdims=False)
        first = lax.index_in_dim(slab, 0, axis=dim, keepdims=False)
        before = lax.ppermute(last, axis, up)
        after = lax.ppermute(first, axis, down)
        head = lax.index_in_dim(slab, 0, axis=dim) + jnp.expand_dims(before, dim)
        tail = lax.index_in_dim(slab, length - 1, axis=dim) + jnp.expand_dims(after, dim)
        middle = lax.slice_in_dim(slab, 1, length - 1, axis=dim)
        slab = jnp.concatenate([head, middle, tail], axis=dim)
    return slab


def assemble(gathered):
    groups, bricks, comps, nbx, nby, nbz = gathered.shape
    highest = lax.Precision.HIGHEST
    place_x = scatter_matrix(bricks, nbx - 1)
    place_z = scatter_matrix(groups, nbz - 1)
    along_x = jnp.einsum("pqcijk,qix->pcxjk", gathered, place_x, precision=highest)
    return jnp.einsum("pcxjk,pkz->cxjz", along_x, place_z, precision=highest)


def local(ref_volume, def_volume, shifts, init_disp, precond):
    width_x, rows_y, depth_z = ref_volume.shape
    dev_count = lax.axis_size("dev")
    grp_count = lax.axis_size("grp")
    grp_index = lax.axis_index("grp")
    dev_index = lax.axis_index("dev")
    voxel_count = float(width_x * rows_y * depth_z * dev_count * grp_count)
    margin = SMAX + 1
    offset = shifts[0, 0]
    widened = with_halo(def_volume, (("dev", 0),), margin)
    up = [(i, i + 1) for i in range(grp_count - 1)]
    down = [(j, i) for i, j in up]
    below = lax.ppermute(widened[:, :, -1:], "grp", up)
    above = lax.ppermute(widened[:, :, :1], "grp", down)
    slopes, sample = native_slopes(offset.reshape(1), widened, below, above, width_x)
    target = ref_volume.astype(jnp.float32)
    elements_x = width_x // E
    elements_z = depth_z // E
    nodes_y = rows_y // E + 1
    hat_x = hat_matrix(width_x, elements_x + 1)
    hat_y = hat_matrix(rows_y, nodes_y)
    hat_z = hat_matrix(depth_z, elements_z + 1)
    corner = (0, dev_index * elements_x, 0, grp_index * elements_z)
    extent = (3, elements_x + 1, nodes_y, elements_z + 1)
    local_nodes = lax.dynamic_slice(init_disp, corner, extent)
    local_precond = lax.dynamic_slice(precond, corner, extent)
    target_sums = jnp.stack([jnp.sum(target), jnp.sum(target * target)])
    residual = target
    total_slab = None
    mean_ref = var_ref = None
    for iteration in range(ITERS):
        shift_field = expand_x(interpolate(local_nodes, hat_y, hat_z), hat_x)
        warped = sample + jnp.sum(shift_field * slopes, axis=0)
        image_sums = jnp.stack([jnp.sum(warped), jnp.sum(warped * warped)])
        if iteration == 0:
            sums = allsum(jnp.concatenate([target_sums, image_sums]))
            mean_ref = sums[0] / voxel_count
            var_ref = sums[1] / voxel_count - mean_ref * mean_ref
            image_sums = sums[2:]
        else:
            image_sums = allsum(image_sums)
        mean_img = image_sums[0] / voxel_count
        var_img = image_sums[1] / voxel_count - mean_img * mean_img
        ratio = jnp.sqrt((var_ref + epsilon) / (var_img + epsilon))
        residual = target - mean_ref - ratio * (warped - mean_img)
        slab = restrict(slopes * residual[None], hat_x, hat_y, hat_z)
        total_slab = slab if total_slab is None else total_slab + slab
        if iteration + 1 < ITERS:
            local_nodes = local_nodes + local_precond * share_nodes(slab)
    squares = jnp.sum(residual * residual)
    packed = jnp.concatenate([total_slab.reshape(-1), squares[None]])
    gathered = lax.all_gather(packed.reshape(2, -1), ("grp", "dev")).reshape(grp_count * dev_count, -1)
    pieces = gathered[:, :-1].reshape((grp_count, dev_count) + total_slab.shape)
    forces = assemble(pieces)
    motion = init_disp + precond * forces
    misfit = jnp.sqrt(jnp.sum(gathered[:, -1]) / voxel_count)
    return (motion, residual, misfit)


def solution(mesh):
    placed = (P("dev", None, "grp"), P("dev", None, "grp"), P("grp", "dev"), P(), P())
    return jax.shard_map(
        local,
        mesh=mesh,
        in_specs=placed,
        out_specs=(P(), P("dev", None, "grp"), P()),
        check_vma=False,
    )
```

```python
import jax
import jax.numpy as jnp
from jax import lax
from jax.sharding import PartitionSpec as P
from jax.experimental import pallas as pl
from jax.experimental.pallas import tpu as pltpu

E = 16
SMAX = 8
ITERS = 2


epsilon = 1e-06


def with_halo(shard, sides, width):
    for axis, dim in sides:
        devices, length = (lax.axis_size(axis), shard.shape[dim])
        up = [(i, (i + 1) % devices) for i in range(devices - 1)]
        down = [(j, i) for i, j in up]
        last = lax.slice_in_dim(shard, length - width, length, axis=dim)
        initial = lax.slice_in_dim(shard, 0, width, axis=dim)
        before = lax.ppermute(last, axis, up)
        after = lax.ppermute(initial, axis, down)
        shard = jnp.concatenate([before, shard, after], axis=dim)
    return shard


from jax.experimental import pallas as pl
from jax.experimental.pallas import tpu as pltpu

PLANES = 8


def _native_kernel(offset_ref, w_ref, lo_ref, hi_ref, sl_ref, sm_ref, keep_ref):
    step = pl.program_id(0)
    _, wy, wz = w_ref.shape
    row = lax.broadcasted_iota(jnp.int32, (wy, wz), 0)
    lane = lax.broadcasted_iota(jnp.int32, (wy, wz), 1)
    sixth = 1.0 / 6.0
    base = offset_ref[0] + SMAX + step * PLANES

    def planes(t):
        p = base + t
        w = w_ref[p].astype(jnp.float32)
        below = jnp.where(lane == 0, lo_ref[p].astype(jnp.float32), pltpu.roll(w, 1, 1))
        above = jnp.where(lane == wz - 1, hi_ref[p].astype(jnp.float32), pltpu.roll(w, wz - 1, 1))
        smooth_z = (below + 4.0 * w + above) * sixth
        differ_z = 0.5 * (above - below)
        s_lo = jnp.where(row == 0, 0.0, pltpu.roll(smooth_z, 1, 0))
        s_hi = jnp.where(row == wy - 1, 0.0, pltpu.roll(smooth_z, wy - 1, 0))
        d_lo = jnp.where(row == 0, 0.0, pltpu.roll(differ_z, 1, 0))
        d_hi = jnp.where(row == wy - 1, 0.0, pltpu.roll(differ_z, wy - 1, 0))
        return (
            (s_lo + 4.0 * smooth_z + s_hi) * sixth,
            0.5 * (s_hi - s_lo),
            (d_lo + 4.0 * differ_z + d_hi) * sixth,
            w,
        )

    @pl.when(step == 0)
    def _():
        for t in range(2):
            for n, value in enumerate(planes(t)):
                keep_ref[t, n] = value

    window = [tuple(keep_ref[t, n] for n in range(4)) for t in range(2)]
    for k in range(PLANES):
        window.append(planes(k + 2))
        prev, mid, nxt = window[k], window[k + 1], window[k + 2]
        sl_ref[0, k] = 0.5 * (nxt[0] - prev[0])
        sl_ref[1, k] = (prev[1] + 4.0 * mid[1] + nxt[1]) * sixth
        sl_ref[2, k] = (prev[2] + 4.0 * mid[2] + nxt[2]) * sixth
        sm_ref[k] = mid[3]
    for t in range(2):
        for n, value in enumerate(window[PLANES + t]):
            keep_ref[t, n] = value


def native_slopes(offset, widened, below, above, width_x, interpret=False):
    _, wy, wz = widened.shape
    assert width_x % PLANES == 0
    whole = pl.BlockSpec(widened.shape, lambda i, o: (0, 0, 0))
    face = pl.BlockSpec(below.shape, lambda i, o: (0, 0, 0))
    spec = pltpu.PrefetchScalarGridSpec(
        num_scalar_prefetch=1,
        grid=(width_x // PLANES,),
        in_specs=[whole, face, face],
        scratch_shapes=[pltpu.VMEM((2, 4, wy, wz), jnp.float32)],
        out_specs=[
            pl.BlockSpec((3, PLANES, wy, wz), lambda i, o: (0, i, 0, 0)),
            pl.BlockSpec((PLANES, wy, wz), lambda i, o: (i, 0, 0)),
        ],
    )
    return pl.pallas_call(
        _native_kernel,
        grid_spec=spec,
        out_shape=[
            jax.ShapeDtypeStruct((3, width_x, wy, wz), jnp.float32),
            jax.ShapeDtypeStruct((width_x, wy, wz), jnp.float32),
        ],
        interpret=interpret,
    )(offset, widened, below, above)


def hat_matrix(voxels, nodes):
    positions = jnp.arange(voxels, dtype=jnp.int32)
    element = positions // E
    fraction = (positions - element * E).astype(jnp.float32) / E
    columns = jnp.arange(nodes, dtype=jnp.int32)
    left_part = (columns[None, :] == element[:, None]).astype(jnp.float32) * (1.0 - fraction)[
        :, None
    ]
    right_part = (columns[None, :] == element[:, None] + 1).astype(jnp.float32) * fraction[:, None]
    return left_part + right_part


def smooth(values, direction):
    extent = values.shape[direction]
    lower = lax.slice_in_dim(values, 0, extent - 2, axis=direction)
    middle = lax.slice_in_dim(values, 1, extent - 1, axis=direction)
    upper = lax.slice_in_dim(values, 2, extent, axis=direction)
    return (lower + 4.0 * middle + upper) / 6.0


def differ(values, direction):
    extent = values.shape[direction]
    lower = lax.slice_in_dim(values, 0, extent - 2, axis=direction)
    upper = lax.slice_in_dim(values, 2, extent, axis=direction)
    return 0.5 * (upper - lower)


def gradients(window):
    smooth_z = smooth(window, 2)
    slope_x = differ(smooth(smooth_z, 1), 0)
    slope_y = smooth(differ(smooth_z, 1), 0)
    slope_z = smooth(smooth(differ(window, 2), 1), 0)
    return jnp.stack([slope_x, slope_y, slope_z])


def interpolate(local_nodes, hat_y, hat_z):
    highest = lax.Precision.HIGHEST
    partial_z = jnp.einsum("cijk,zk->cijz", local_nodes, hat_z, precision=highest)
    return jnp.einsum("cijz,yj->ciyz", partial_z, hat_y, precision=highest)


def expand_x(partial_y, hat_x):
    return sum(
        hat_x[None, :, i, None, None] * partial_y[:, i, None] for i in range(hat_x.shape[1])
    )


def restrict(terms, hat_x, hat_y, hat_z):
    highest = lax.Precision.HIGHEST
    partial_x = jnp.stack(
        [jnp.sum(terms * hat_x[None, :, i, None, None], axis=1) for i in range(hat_x.shape[1])],
        axis=1,
    )
    partial_y = jnp.einsum("ciyz,yj->cijz", partial_x, hat_y, precision=highest)
    return jnp.einsum("cijz,zk->cijk", partial_y, hat_z, precision=highest)


def scatter_matrix(bricks, elements):
    columns = jnp.arange(bricks * elements + 1, dtype=jnp.int32)
    starts = jnp.arange(bricks, dtype=jnp.int32)[:, None] * elements
    rows = starts + jnp.arange(elements + 1, dtype=jnp.int32)[None, :]
    return (rows[:, :, None] == columns[None, None, :]).astype(jnp.float32)


def allsum(values):
    for axis in ("dev", "grp"):
        devices = lax.axis_size(axis)
        assert devices & (devices - 1) == 0
        step = 1
        while step < devices:
            pairs = [(i, i ^ step) for i in range(devices)]
            values = values + lax.ppermute(values, axis, pairs)
            step *= 2
    return values


def share_nodes(slab):
    for axis, dim in (("dev", 1), ("grp", 3)):
        devices, length = (lax.axis_size(axis), slab.shape[dim])
        up = [(i, i + 1) for i in range(devices - 1)]
        down = [(j, i) for i, j in up]
        last = lax.index_in_dim(slab, length - 1, axis=dim, keepdims=False)
        first = lax.index_in_dim(slab, 0, axis=dim, keepdims=False)
        before = lax.ppermute(last, axis, up)
        after = lax.ppermute(first, axis, down)
        head = lax.index_in_dim(slab, 0, axis=dim) + jnp.expand_dims(before, dim)
        tail = lax.index_in_dim(slab, length - 1, axis=dim) + jnp.expand_dims(after, dim)
        middle = lax.slice_in_dim(slab, 1, length - 1, axis=dim)
        slab = jnp.concatenate([head, middle, tail], axis=dim)
    return slab


def assemble(gathered):
    groups, bricks, comps, nbx, nby, nbz = gathered.shape
    highest = lax.Precision.HIGHEST
    place_x = scatter_matrix(bricks, nbx - 1)
    place_z = scatter_matrix(groups, nbz - 1)
    along_x = jnp.einsum("pqcijk,qix->pcxjk", gathered, place_x, precision=highest)
    return jnp.einsum("pcxjk,pkz->cxjz", along_x, place_z, precision=highest)


def local(ref_volume, def_volume, shifts, init_disp, precond):
    width_x, rows_y, depth_z = ref_volume.shape
    dev_count = lax.axis_size("dev")
    grp_count = lax.axis_size("grp")
    grp_index = lax.axis_index("grp")
    dev_index = lax.axis_index("dev")
    voxel_count = float(width_x * rows_y * depth_z * dev_count * grp_count)
    margin = SMAX + 1
    offset = shifts[0, 0]
    widened = with_halo(def_volume, (("dev", 0),), margin)
    up = [(i, i + 1) for i in range(grp_count - 1)]
    down = [(j, i) for i, j in up]
    below = lax.ppermute(widened[:, :, -1:], "grp", up)
    above = lax.ppermute(widened[:, :, :1], "grp", down)
    slopes, sample = native_slopes(offset.reshape(1), widened, below, above, width_x)
    target = ref_volume.astype(jnp.float32)
    elements_x = width_x // E
    elements_z = depth_z // E
    nodes_y = rows_y // E + 1
    hat_x = hat_matrix(width_x, elements_x + 1)
    hat_y = hat_matrix(rows_y, nodes_y)
    hat_z = hat_matrix(depth_z, elements_z + 1)
    corner = (0, dev_index * elements_x, 0, grp_index * elements_z)
    extent = (3, elements_x + 1, nodes_y, elements_z + 1)
    local_nodes = lax.dynamic_slice(init_disp, corner, extent)
    local_precond = lax.dynamic_slice(precond, corner, extent)
    target_sums = jnp.stack([jnp.sum(target), jnp.sum(target * target)])
    residual = target
    total_slab = None
    mean_ref = var_ref = None
    for iteration in range(ITERS):
        shift_field = expand_x(interpolate(local_nodes, hat_y, hat_z), hat_x)
        warped = sample + jnp.sum(shift_field * slopes, axis=0)
        image_sums = jnp.stack([jnp.sum(warped), jnp.sum(warped * warped)])
        if iteration == 0:
            sums = allsum(jnp.concatenate([target_sums, image_sums]))
            mean_ref = sums[0] / voxel_count
            var_ref = sums[1] / voxel_count - mean_ref * mean_ref
            image_sums = sums[2:]
        else:
            image_sums = allsum(image_sums)
        mean_img = image_sums[0] / voxel_count
        var_img = image_sums[1] / voxel_count - mean_img * mean_img
        ratio = jnp.sqrt((var_ref + epsilon) / (var_img + epsilon))
        residual = target - mean_ref - ratio * (warped - mean_img)
        slab = restrict(slopes * residual[None], hat_x, hat_y, hat_z)
        total_slab = slab if total_slab is None else total_slab + slab
        if iteration + 1 < ITERS:
            local_nodes = local_nodes + local_precond * share_nodes(slab)
    squares = jnp.sum(residual * residual)
    packed = jnp.concatenate([total_slab.reshape(-1), squares[None]])
    gathered = lax.all_gather(packed.reshape(2, -1), ("grp", "dev")).reshape(grp_count * dev_count, -1)
    pieces = gathered[:, :-1].reshape((grp_count, dev_count) + total_slab.shape)
    forces = assemble(pieces)
    motion = init_disp + precond * forces
    misfit = jnp.sqrt(jnp.sum(gathered[:, -1]) / voxel_count)
    return (motion, residual, misfit)


def solution(mesh):
    placed = (P("dev", None, "grp"), P("dev", None, "grp"), P("grp", "dev"), P(), P())
    return jax.shard_map(
        local,
        mesh=mesh,
        in_specs=placed,
        out_specs=(P(), P("dev", None, "grp"), P()),
        check_vma=False,
    )
```

```python
import jax
import jax.numpy as jnp
from jax import lax
from jax.sharding import PartitionSpec as P
from jax.experimental import pallas as pl
from jax.experimental.pallas import tpu as pltpu

E = 16
SMAX = 8
ITERS = 2


epsilon = 1e-06


def with_halo(shard, sides, width):
    for axis, dim in sides:
        devices, length = (lax.axis_size(axis), shard.shape[dim])
        up = [(i, (i + 1) % devices) for i in range(devices - 1)]
        down = [(j, i) for i, j in up]
        last = lax.slice_in_dim(shard, length - width, length, axis=dim)
        initial = lax.slice_in_dim(shard, 0, width, axis=dim)
        before = lax.ppermute(last, axis, up)
        after = lax.ppermute(initial, axis, down)
        shard = jnp.concatenate([before, shard, after], axis=dim)
    return shard


from jax.experimental import pallas as pl
from jax.experimental.pallas import tpu as pltpu

PLANES = 8


def _native_kernel(offset_ref, w_ref, lo_ref, hi_ref, q_ref, sl_ref, wp_ref, mo_ref, keep_ref):
    step = pl.program_id(0)
    _, wy, wz = w_ref.shape
    row = lax.broadcasted_iota(jnp.int32, (wy, wz), 0)
    lane = lax.broadcasted_iota(jnp.int32, (wy, wz), 1)
    sixth = 1.0 / 6.0
    base = offset_ref[0] + SMAX + step * PLANES

    def planes(t):
        p = base + t
        w = w_ref[p].astype(jnp.float32)
        below = jnp.where(lane == 0, lo_ref[p].astype(jnp.float32), pltpu.roll(w, 1, 1))
        above = jnp.where(lane == wz - 1, hi_ref[p].astype(jnp.float32), pltpu.roll(w, wz - 1, 1))
        smooth_z = (below + 4.0 * w + above) * sixth
        differ_z = 0.5 * (above - below)
        s_lo = jnp.where(row == 0, 0.0, pltpu.roll(smooth_z, 1, 0))
        s_hi = jnp.where(row == wy - 1, 0.0, pltpu.roll(smooth_z, wy - 1, 0))
        d_lo = jnp.where(row == 0, 0.0, pltpu.roll(differ_z, 1, 0))
        d_hi = jnp.where(row == wy - 1, 0.0, pltpu.roll(differ_z, wy - 1, 0))
        return (
            (s_lo + 4.0 * smooth_z + s_hi) * sixth,
            0.5 * (s_hi - s_lo),
            (d_lo + 4.0 * differ_z + d_hi) * sixth,
            w,
        )

    @pl.when(step == 0)
    def _():
        mo_ref[...] = jnp.zeros(mo_ref.shape, jnp.float32)
        for t in range(2):
            for n, value in enumerate(planes(t)):
                keep_ref[t, n] = value

    window = [tuple(keep_ref[t, n] for n in range(4)) for t in range(2)]
    total, square = mo_ref[0], mo_ref[1]
    for k in range(PLANES):
        window.append(planes(k + 2))
        prev, mid, nxt = window[k], window[k + 1], window[k + 2]
        slopes = (
            0.5 * (nxt[0] - prev[0]),
            (prev[1] + 4.0 * mid[1] + nxt[1]) * sixth,
            (prev[2] + 4.0 * mid[2] + nxt[2]) * sixth,
        )
        x = step * PLANES + k
        node = x // E
        part = (x - node * E).astype(jnp.float32) / E
        warped = mid[3]
        moved = None
        for c in range(3):
            sl_ref[c, k] = slopes[c]
            field = (1.0 - part) * q_ref[c, node] + part * q_ref[c, node + 1]
            moved = field * slopes[c] if moved is None else moved + field * slopes[c]
        warped = warped + moved
        wp_ref[k] = warped
        total = total + warped
        square = square + warped * warped
    mo_ref[0] = total
    mo_ref[1] = square
    for t in range(2):
        for n, value in enumerate(window[PLANES + t]):
            keep_ref[t, n] = value


def native_slopes(offset, widened, below, above, partial, width_x, interpret=False):
    _, wy, wz = widened.shape
    assert width_x % PLANES == 0
    whole = pl.BlockSpec(widened.shape, lambda i, o: (0, 0, 0))
    face = pl.BlockSpec(below.shape, lambda i, o: (0, 0, 0))
    spec = pltpu.PrefetchScalarGridSpec(
        num_scalar_prefetch=1,
        grid=(width_x // PLANES,),
        in_specs=[whole, face, face, pl.BlockSpec(partial.shape, lambda i, o: (0, 0, 0, 0))],
        scratch_shapes=[pltpu.VMEM((2, 4, wy, wz), jnp.float32)],
        out_specs=[
            pl.BlockSpec((3, PLANES, wy, wz), lambda i, o: (0, i, 0, 0)),
            pl.BlockSpec((PLANES, wy, wz), lambda i, o: (i, 0, 0)),
            pl.BlockSpec((2, wy, wz), lambda i, o: (0, 0, 0)),
        ],
    )
    return pl.pallas_call(
        _native_kernel,
        grid_spec=spec,
        out_shape=[
            jax.ShapeDtypeStruct((3, width_x, wy, wz), jnp.float32),
            jax.ShapeDtypeStruct((width_x, wy, wz), jnp.float32),
            jax.ShapeDtypeStruct((2, wy, wz), jnp.float32),
        ],
        interpret=interpret,
    )(offset, widened, below, above, partial)


def hat_matrix(voxels, nodes):
    positions = jnp.arange(voxels, dtype=jnp.int32)
    element = positions // E
    fraction = (positions - element * E).astype(jnp.float32) / E
    columns = jnp.arange(nodes, dtype=jnp.int32)
    left_part = (columns[None, :] == element[:, None]).astype(jnp.float32) * (1.0 - fraction)[
        :, None
    ]
    right_part = (columns[None, :] == element[:, None] + 1).astype(jnp.float32) * fraction[:, None]
    return left_part + right_part


def smooth(values, direction):
    extent = values.shape[direction]
    lower = lax.slice_in_dim(values, 0, extent - 2, axis=direction)
    middle = lax.slice_in_dim(values, 1, extent - 1, axis=direction)
    upper = lax.slice_in_dim(values, 2, extent, axis=direction)
    return (lower + 4.0 * middle + upper) / 6.0


def differ(values, direction):
    extent = values.shape[direction]
    lower = lax.slice_in_dim(values, 0, extent - 2, axis=direction)
    upper = lax.slice_in_dim(values, 2, extent, axis=direction)
    return 0.5 * (upper - lower)


def gradients(window):
    smooth_z = smooth(window, 2)
    slope_x = differ(smooth(smooth_z, 1), 0)
    slope_y = smooth(differ(smooth_z, 1), 0)
    slope_z = smooth(smooth(differ(window, 2), 1), 0)
    return jnp.stack([slope_x, slope_y, slope_z])


def interpolate(local_nodes, hat_y, hat_z):
    highest = lax.Precision.HIGHEST
    partial_z = jnp.einsum("cijk,zk->cijz", local_nodes, hat_z, precision=highest)
    return jnp.einsum("cijz,yj->ciyz", partial_z, hat_y, precision=highest)


def expand_x(partial_y, hat_x):
    return sum(
        hat_x[None, :, i, None, None] * partial_y[:, i, None] for i in range(hat_x.shape[1])
    )


def restrict(terms, hat_x, hat_y, hat_z):
    highest = lax.Precision.HIGHEST
    partial_x = jnp.stack(
        [jnp.sum(terms * hat_x[None, :, i, None, None], axis=1) for i in range(hat_x.shape[1])],
        axis=1,
    )
    partial_y = jnp.einsum("ciyz,yj->cijz", partial_x, hat_y, precision=highest)
    return jnp.einsum("cijz,zk->cijk", partial_y, hat_z, precision=highest)


def scatter_matrix(bricks, elements):
    columns = jnp.arange(bricks * elements + 1, dtype=jnp.int32)
    starts = jnp.arange(bricks, dtype=jnp.int32)[:, None] * elements
    rows = starts + jnp.arange(elements + 1, dtype=jnp.int32)[None, :]
    return (rows[:, :, None] == columns[None, None, :]).astype(jnp.float32)


def allsum(values):
    for axis in ("dev", "grp"):
        devices = lax.axis_size(axis)
        assert devices & (devices - 1) == 0
        step = 1
        while step < devices:
            pairs = [(i, i ^ step) for i in range(devices)]
            values = values + lax.ppermute(values, axis, pairs)
            step *= 2
    return values


def share_nodes(slab):
    for axis, dim in (("dev", 1), ("grp", 3)):
        devices, length = (lax.axis_size(axis), slab.shape[dim])
        up = [(i, i + 1) for i in range(devices - 1)]
        down = [(j, i) for i, j in up]
        last = lax.index_in_dim(slab, length - 1, axis=dim, keepdims=False)
        first = lax.index_in_dim(slab, 0, axis=dim, keepdims=False)
        before = lax.ppermute(last, axis, up)
        after = lax.ppermute(first, axis, down)
        head = lax.index_in_dim(slab, 0, axis=dim) + jnp.expand_dims(before, dim)
        tail = lax.index_in_dim(slab, length - 1, axis=dim) + jnp.expand_dims(after, dim)
        middle = lax.slice_in_dim(slab, 1, length - 1, axis=dim)
        slab = jnp.concatenate([head, middle, tail], axis=dim)
    return slab


def assemble(gathered):
    groups, bricks, comps, nbx, nby, nbz = gathered.shape
    highest = lax.Precision.HIGHEST
    place_x = scatter_matrix(bricks, nbx - 1)
    place_z = scatter_matrix(groups, nbz - 1)
    along_x = jnp.einsum("pqcijk,qix->pcxjk", gathered, place_x, precision=highest)
    return jnp.einsum("pcxjk,pkz->cxjz", along_x, place_z, precision=highest)


def local(ref_volume, def_volume, shifts, init_disp, precond):
    width_x, rows_y, depth_z = ref_volume.shape
    dev_count = lax.axis_size("dev")
    grp_count = lax.axis_size("grp")
    grp_index = lax.axis_index("grp")
    dev_index = lax.axis_index("dev")
    voxel_count = float(width_x * rows_y * depth_z * dev_count * grp_count)
    margin = SMAX + 1
    offset = shifts[0, 0]
    widened = with_halo(def_volume, (("dev", 0),), margin)
    up = [(i, i + 1) for i in range(grp_count - 1)]
    down = [(j, i) for i, j in up]
    below = lax.ppermute(widened[:, :, -1:], "grp", up)
    above = lax.ppermute(widened[:, :, :1], "grp", down)
    target = ref_volume.astype(jnp.float32)
    elements_x = width_x // E
    elements_z = depth_z // E
    nodes_y = rows_y // E + 1
    hat_x = hat_matrix(width_x, elements_x + 1)
    hat_y = hat_matrix(rows_y, nodes_y)
    hat_z = hat_matrix(depth_z, elements_z + 1)
    corner = (0, dev_index * elements_x, 0, grp_index * elements_z)
    extent = (3, elements_x + 1, nodes_y, elements_z + 1)
    local_nodes = lax.dynamic_slice(init_disp, corner, extent)
    local_precond = lax.dynamic_slice(precond, corner, extent)
    target_sums = jnp.stack([jnp.sum(target), jnp.sum(target * target)])
    partial = interpolate(local_nodes, hat_y, hat_z)
    slopes, warped, moments = native_slopes(
        offset.reshape(1), widened, below, above, partial, width_x
    )
    residual = target
    total_slab = None
    mean_ref = var_ref = None
    for iteration in range(ITERS):
        if iteration == 0:
            image_sums = jnp.sum(moments, axis=(1, 2))
        else:
            moved = interpolate(local_nodes, hat_y, hat_z)
            shift_field = expand_x(moved - partial, hat_x)
            warped = warped + jnp.sum(shift_field * slopes, axis=0)
            partial = moved
            image_sums = jnp.stack([jnp.sum(warped), jnp.sum(warped * warped)])
        if iteration == 0:
            sums = allsum(jnp.concatenate([target_sums, image_sums]))
            mean_ref = sums[0] / voxel_count
            var_ref = sums[1] / voxel_count - mean_ref * mean_ref
            image_sums = sums[2:]
        else:
            image_sums = allsum(image_sums)
        mean_img = image_sums[0] / voxel_count
        var_img = image_sums[1] / voxel_count - mean_img * mean_img
        ratio = jnp.sqrt((var_ref + epsilon) / (var_img + epsilon))
        residual = target - mean_ref - ratio * (warped - mean_img)
        slab = restrict(slopes * residual[None], hat_x, hat_y, hat_z)
        total_slab = slab if total_slab is None else total_slab + slab
        if iteration + 1 < ITERS:
            local_nodes = local_nodes + local_precond * share_nodes(slab)
    squares = jnp.sum(residual * residual)
    packed = jnp.concatenate([total_slab.reshape(-1), squares[None]])
    gathered = lax.all_gather(packed.reshape(2, -1), ("grp", "dev")).reshape(grp_count * dev_count, -1)
    pieces = gathered[:, :-1].reshape((grp_count, dev_count) + total_slab.shape)
    forces = assemble(pieces)
    motion = init_disp + precond * forces
    misfit = jnp.sqrt(jnp.sum(gathered[:, -1]) / voxel_count)
    return (motion, residual, misfit)


def solution(mesh):
    placed = (P("dev", None, "grp"), P("dev", None, "grp"), P("grp", "dev"), P(), P())
    return jax.shard_map(
        local,
        mesh=mesh,
        in_specs=placed,
        out_specs=(P(), P("dev", None, "grp"), P()),
        check_vma=False,
    )
```

```python
import jax
import jax.numpy as jnp
from jax import lax
from jax.sharding import PartitionSpec as P
from jax.experimental import pallas as pl
from jax.experimental.pallas import tpu as pltpu

E = 16
SMAX = 8
ITERS = 2


epsilon = 1e-06


def with_halo(shard, sides, width):
    for axis, dim in sides:
        devices, length = (lax.axis_size(axis), shard.shape[dim])
        up = [(i, (i + 1) % devices) for i in range(devices - 1)]
        down = [(j, i) for i, j in up]
        last = lax.slice_in_dim(shard, length - width, length, axis=dim)
        initial = lax.slice_in_dim(shard, 0, width, axis=dim)
        before = lax.ppermute(last, axis, up)
        after = lax.ppermute(initial, axis, down)
        shard = jnp.concatenate([before, shard, after], axis=dim)
    return shard


from jax.experimental import pallas as pl
from jax.experimental.pallas import tpu as pltpu

PLANES = 4


def _native_kernel(offset_ref, w_ref, lo_ref, hi_ref, sl_ref, sm_ref, keep_ref):
    step = pl.program_id(0)
    _, wy, wz = w_ref.shape
    row = lax.broadcasted_iota(jnp.int32, (wy, wz), 0)
    lane = lax.broadcasted_iota(jnp.int32, (wy, wz), 1)
    sixth = 1.0 / 6.0
    base = offset_ref[0] + SMAX + step * PLANES

    def planes(t):
        p = base + t
        w = w_ref[p].astype(jnp.float32)
        below = jnp.where(lane == 0, lo_ref[p].astype(jnp.float32), pltpu.roll(w, 1, 1))
        above = jnp.where(lane == wz - 1, hi_ref[p].astype(jnp.float32), pltpu.roll(w, wz - 1, 1))
        smooth_z = (below + 4.0 * w + above) * sixth
        differ_z = 0.5 * (above - below)
        s_lo = jnp.where(row == 0, 0.0, pltpu.roll(smooth_z, 1, 0))
        s_hi = jnp.where(row == wy - 1, 0.0, pltpu.roll(smooth_z, wy - 1, 0))
        d_lo = jnp.where(row == 0, 0.0, pltpu.roll(differ_z, 1, 0))
        d_hi = jnp.where(row == wy - 1, 0.0, pltpu.roll(differ_z, wy - 1, 0))
        return (
            (s_lo + 4.0 * smooth_z + s_hi) * sixth,
            0.5 * (s_hi - s_lo),
            (d_lo + 4.0 * differ_z + d_hi) * sixth,
            w,
        )

    @pl.when(step == 0)
    def _():
        for t in range(2):
            for n, value in enumerate(planes(t)):
                keep_ref[t, n] = value

    window = [tuple(keep_ref[t, n] for n in range(4)) for t in range(2)]
    for k in range(PLANES):
        window.append(planes(k + 2))
        prev, mid, nxt = window[k], window[k + 1], window[k + 2]
        sl_ref[0, k] = 0.5 * (nxt[0] - prev[0])
        sl_ref[1, k] = (prev[1] + 4.0 * mid[1] + nxt[1]) * sixth
        sl_ref[2, k] = (prev[2] + 4.0 * mid[2] + nxt[2]) * sixth
        sm_ref[k] = mid[3]
    for t in range(2):
        for n, value in enumerate(window[PLANES + t]):
            keep_ref[t, n] = value


def native_slopes(offset, widened, below, above, width_x, interpret=False):
    _, wy, wz = widened.shape
    assert width_x % PLANES == 0
    whole = pl.BlockSpec(widened.shape, lambda i, o: (0, 0, 0))
    face = pl.BlockSpec(below.shape, lambda i, o: (0, 0, 0))
    spec = pltpu.PrefetchScalarGridSpec(
        num_scalar_prefetch=1,
        grid=(width_x // PLANES,),
        in_specs=[whole, face, face],
        scratch_shapes=[pltpu.VMEM((2, 4, wy, wz), jnp.float32)],
        out_specs=[
            pl.BlockSpec((3, PLANES, wy, wz), lambda i, o: (0, i, 0, 0)),
            pl.BlockSpec((PLANES, wy, wz), lambda i, o: (i, 0, 0)),
        ],
    )
    return pl.pallas_call(
        _native_kernel,
        grid_spec=spec,
        out_shape=[
            jax.ShapeDtypeStruct((3, width_x, wy, wz), jnp.float32),
            jax.ShapeDtypeStruct((width_x, wy, wz), jnp.float32),
        ],
        interpret=interpret,
    )(offset, widened, below, above)


def hat_matrix(voxels, nodes):
    positions = jnp.arange(voxels, dtype=jnp.int32)
    element = positions // E
    fraction = (positions - element * E).astype(jnp.float32) / E
    columns = jnp.arange(nodes, dtype=jnp.int32)
    left_part = (columns[None, :] == element[:, None]).astype(jnp.float32) * (1.0 - fraction)[
        :, None
    ]
    right_part = (columns[None, :] == element[:, None] + 1).astype(jnp.float32) * fraction[:, None]
    return left_part + right_part


def smooth(values, direction):
    extent = values.shape[direction]
    lower = lax.slice_in_dim(values, 0, extent - 2, axis=direction)
    middle = lax.slice_in_dim(values, 1, extent - 1, axis=direction)
    upper = lax.slice_in_dim(values, 2, extent, axis=direction)
    return (lower + 4.0 * middle + upper) / 6.0


def differ(values, direction):
    extent = values.shape[direction]
    lower = lax.slice_in_dim(values, 0, extent - 2, axis=direction)
    upper = lax.slice_in_dim(values, 2, extent, axis=direction)
    return 0.5 * (upper - lower)


def gradients(window):
    smooth_z = smooth(window, 2)
    slope_x = differ(smooth(smooth_z, 1), 0)
    slope_y = smooth(differ(smooth_z, 1), 0)
    slope_z = smooth(smooth(differ(window, 2), 1), 0)
    return jnp.stack([slope_x, slope_y, slope_z])


def interpolate(local_nodes, hat_y, hat_z):
    highest = lax.Precision.HIGHEST
    partial_z = jnp.einsum("cijk,zk->cijz", local_nodes, hat_z, precision=highest)
    return jnp.einsum("cijz,yj->ciyz", partial_z, hat_y, precision=highest)


def expand_x(partial_y, hat_x):
    return sum(
        hat_x[None, :, i, None, None] * partial_y[:, i, None] for i in range(hat_x.shape[1])
    )


def restrict(terms, hat_x, hat_y, hat_z):
    highest = lax.Precision.HIGHEST
    partial_x = jnp.stack(
        [jnp.sum(terms * hat_x[None, :, i, None, None], axis=1) for i in range(hat_x.shape[1])],
        axis=1,
    )
    partial_y = jnp.einsum("ciyz,yj->cijz", partial_x, hat_y, precision=highest)
    return jnp.einsum("cijz,zk->cijk", partial_y, hat_z, precision=highest)


def scatter_matrix(bricks, elements):
    columns = jnp.arange(bricks * elements + 1, dtype=jnp.int32)
    starts = jnp.arange(bricks, dtype=jnp.int32)[:, None] * elements
    rows = starts + jnp.arange(elements + 1, dtype=jnp.int32)[None, :]
    return (rows[:, :, None] == columns[None, None, :]).astype(jnp.float32)


def allsum(values):
    for axis in ("dev", "grp"):
        devices = lax.axis_size(axis)
        assert devices & (devices - 1) == 0
        step = 1
        while step < devices:
            pairs = [(i, i ^ step) for i in range(devices)]
            values = values + lax.ppermute(values, axis, pairs)
            step *= 2
    return values


def share_nodes(slab):
    for axis, dim in (("dev", 1), ("grp", 3)):
        devices, length = (lax.axis_size(axis), slab.shape[dim])
        up = [(i, i + 1) for i in range(devices - 1)]
        down = [(j, i) for i, j in up]
        last = lax.index_in_dim(slab, length - 1, axis=dim, keepdims=False)
        first = lax.index_in_dim(slab, 0, axis=dim, keepdims=False)
        before = lax.ppermute(last, axis, up)
        after = lax.ppermute(first, axis, down)
        head = lax.index_in_dim(slab, 0, axis=dim) + jnp.expand_dims(before, dim)
        tail = lax.index_in_dim(slab, length - 1, axis=dim) + jnp.expand_dims(after, dim)
        middle = lax.slice_in_dim(slab, 1, length - 1, axis=dim)
        slab = jnp.concatenate([head, middle, tail], axis=dim)
    return slab


def assemble(gathered):
    groups, bricks, comps, nbx, nby, nbz = gathered.shape
    highest = lax.Precision.HIGHEST
    place_x = scatter_matrix(bricks, nbx - 1)
    place_z = scatter_matrix(groups, nbz - 1)
    along_x = jnp.einsum("pqcijk,qix->pcxjk", gathered, place_x, precision=highest)
    return jnp.einsum("pcxjk,pkz->cxjz", along_x, place_z, precision=highest)


def local(ref_volume, def_volume, shifts, init_disp, precond):
    width_x, rows_y, depth_z = ref_volume.shape
    dev_count = lax.axis_size("dev")
    grp_count = lax.axis_size("grp")
    grp_index = lax.axis_index("grp")
    dev_index = lax.axis_index("dev")
    voxel_count = float(width_x * rows_y * depth_z * dev_count * grp_count)
    margin = SMAX + 1
    offset = shifts[0, 0]
    widened = with_halo(def_volume, (("dev", 0),), margin)
    up = [(i, i + 1) for i in range(grp_count - 1)]
    down = [(j, i) for i, j in up]
    below = lax.ppermute(widened[:, :, -1:], "grp", up)
    above = lax.ppermute(widened[:, :, :1], "grp", down)
    slopes, sample = native_slopes(offset.reshape(1), widened, below, above, width_x)
    target = ref_volume.astype(jnp.float32)
    elements_x = width_x // E
    elements_z = depth_z // E
    nodes_y = rows_y // E + 1
    hat_x = hat_matrix(width_x, elements_x + 1)
    hat_y = hat_matrix(rows_y, nodes_y)
    hat_z = hat_matrix(depth_z, elements_z + 1)
    corner = (0, dev_index * elements_x, 0, grp_index * elements_z)
    extent = (3, elements_x + 1, nodes_y, elements_z + 1)
    local_nodes = lax.dynamic_slice(init_disp, corner, extent)
    local_precond = lax.dynamic_slice(precond, corner, extent)
    target_sums = jnp.stack([jnp.sum(target), jnp.sum(target * target)])
    residual = target
    total_slab = None
    mean_ref = var_ref = None
    for iteration in range(ITERS):
        shift_field = expand_x(interpolate(local_nodes, hat_y, hat_z), hat_x)
        warped = sample + jnp.sum(shift_field * slopes, axis=0)
        image_sums = jnp.stack([jnp.sum(warped), jnp.sum(warped * warped)])
        if iteration == 0:
            sums = allsum(jnp.concatenate([target_sums, image_sums]))
            mean_ref = sums[0] / voxel_count
            var_ref = sums[1] / voxel_count - mean_ref * mean_ref
            image_sums = sums[2:]
        else:
            image_sums = allsum(image_sums)
        mean_img = image_sums[0] / voxel_count
        var_img = image_sums[1] / voxel_count - mean_img * mean_img
        ratio = jnp.sqrt((var_ref + epsilon) / (var_img + epsilon))
        residual = target - mean_ref - ratio * (warped - mean_img)
        slab = restrict(slopes * residual[None], hat_x, hat_y, hat_z)
        total_slab = slab if total_slab is None else total_slab + slab
        if iteration + 1 < ITERS:
            local_nodes = local_nodes + local_precond * share_nodes(slab)
    squares = jnp.sum(residual * residual)
    packed = jnp.concatenate([total_slab.reshape(-1), squares[None]])
    gathered = lax.all_gather(packed.reshape(2, -1), ("grp", "dev")).reshape(grp_count * dev_count, -1)
    pieces = gathered[:, :-1].reshape((grp_count, dev_count) + total_slab.shape)
    forces = assemble(pieces)
    motion = init_disp + precond * forces
    misfit = jnp.sqrt(jnp.sum(gathered[:, -1]) / voxel_count)
    return (motion, residual, misfit)


def solution(mesh):
    placed = (P("dev", None, "grp"), P("dev", None, "grp"), P("grp", "dev"), P(), P())
    return jax.shard_map(
        local,
        mesh=mesh,
        in_specs=placed,
        out_specs=(P(), P("dev", None, "grp"), P()),
        check_vma=False,
    )
```

```python
import jax
import jax.numpy as jnp
from jax import lax
from jax.sharding import PartitionSpec as P
from jax.experimental import pallas as pl
from jax.experimental.pallas import tpu as pltpu

E = 16
SMAX = 8
ITERS = 2


epsilon = 1e-06


def with_halo(shard, sides, width):
    for axis, dim in sides:
        devices, length = (lax.axis_size(axis), shard.shape[dim])
        up = [(i, (i + 1) % devices) for i in range(devices - 1)]
        down = [(j, i) for i, j in up]
        last = lax.slice_in_dim(shard, length - width, length, axis=dim)
        initial = lax.slice_in_dim(shard, 0, width, axis=dim)
        before = lax.ppermute(last, axis, up)
        after = lax.ppermute(initial, axis, down)
        shard = jnp.concatenate([before, shard, after], axis=dim)
    return shard


from jax.experimental import pallas as pl
from jax.experimental.pallas import tpu as pltpu

PLANES = 4


def _native_kernel(offset_ref, w_ref, lo_ref, hi_ref, q_ref, sl_ref, wp_ref, mo_ref, keep_ref):
    step = pl.program_id(0)
    _, wy, wz = w_ref.shape
    row = lax.broadcasted_iota(jnp.int32, (wy, wz), 0)
    lane = lax.broadcasted_iota(jnp.int32, (wy, wz), 1)
    sixth = 1.0 / 6.0
    base = offset_ref[0] + SMAX + step * PLANES

    def planes(t):
        p = base + t
        w = w_ref[p].astype(jnp.float32)
        below = jnp.where(lane == 0, lo_ref[p].astype(jnp.float32), pltpu.roll(w, 1, 1))
        above = jnp.where(lane == wz - 1, hi_ref[p].astype(jnp.float32), pltpu.roll(w, wz - 1, 1))
        smooth_z = (below + 4.0 * w + above) * sixth
        differ_z = 0.5 * (above - below)
        s_lo = jnp.where(row == 0, 0.0, pltpu.roll(smooth_z, 1, 0))
        s_hi = jnp.where(row == wy - 1, 0.0, pltpu.roll(smooth_z, wy - 1, 0))
        d_lo = jnp.where(row == 0, 0.0, pltpu.roll(differ_z, 1, 0))
        d_hi = jnp.where(row == wy - 1, 0.0, pltpu.roll(differ_z, wy - 1, 0))
        return (
            (s_lo + 4.0 * smooth_z + s_hi) * sixth,
            0.5 * (s_hi - s_lo),
            (d_lo + 4.0 * differ_z + d_hi) * sixth,
            w,
        )

    @pl.when(step == 0)
    def _():
        mo_ref[...] = jnp.zeros(mo_ref.shape, jnp.float32)
        for t in range(2):
            for n, value in enumerate(planes(t)):
                keep_ref[t, n] = value

    window = [tuple(keep_ref[t, n] for n in range(4)) for t in range(2)]
    total, square = mo_ref[0], mo_ref[1]
    for k in range(PLANES):
        window.append(planes(k + 2))
        prev, mid, nxt = window[k], window[k + 1], window[k + 2]
        slopes = (
            0.5 * (nxt[0] - prev[0]),
            (prev[1] + 4.0 * mid[1] + nxt[1]) * sixth,
            (prev[2] + 4.0 * mid[2] + nxt[2]) * sixth,
        )
        x = step * PLANES + k
        node = x // E
        part = (x - node * E).astype(jnp.float32) / E
        warped = mid[3]
        moved = None
        for c in range(3):
            sl_ref[c, k] = slopes[c]
            field = (1.0 - part) * q_ref[c, node] + part * q_ref[c, node + 1]
            moved = field * slopes[c] if moved is None else moved + field * slopes[c]
        warped = warped + moved
        wp_ref[k] = warped
        total = total + warped
        square = square + warped * warped
    mo_ref[0] = total
    mo_ref[1] = square
    for t in range(2):
        for n, value in enumerate(window[PLANES + t]):
            keep_ref[t, n] = value


def native_slopes(offset, widened, below, above, partial, width_x, interpret=False):
    _, wy, wz = widened.shape
    assert width_x % PLANES == 0
    whole = pl.BlockSpec(widened.shape, lambda i, o: (0, 0, 0))
    face = pl.BlockSpec(below.shape, lambda i, o: (0, 0, 0))
    spec = pltpu.PrefetchScalarGridSpec(
        num_scalar_prefetch=1,
        grid=(width_x // PLANES,),
        in_specs=[whole, face, face, pl.BlockSpec(partial.shape, lambda i, o: (0, 0, 0, 0))],
        scratch_shapes=[pltpu.VMEM((2, 4, wy, wz), jnp.float32)],
        out_specs=[
            pl.BlockSpec((3, PLANES, wy, wz), lambda i, o: (0, i, 0, 0)),
            pl.BlockSpec((PLANES, wy, wz), lambda i, o: (i, 0, 0)),
            pl.BlockSpec((2, wy, wz), lambda i, o: (0, 0, 0)),
        ],
    )
    return pl.pallas_call(
        _native_kernel,
        grid_spec=spec,
        out_shape=[
            jax.ShapeDtypeStruct((3, width_x, wy, wz), jnp.float32),
            jax.ShapeDtypeStruct((width_x, wy, wz), jnp.float32),
            jax.ShapeDtypeStruct((2, wy, wz), jnp.float32),
        ],
        interpret=interpret,
    )(offset, widened, below, above, partial)


def hat_matrix(voxels, nodes):
    positions = jnp.arange(voxels, dtype=jnp.int32)
    element = positions // E
    fraction = (positions - element * E).astype(jnp.float32) / E
    columns = jnp.arange(nodes, dtype=jnp.int32)
    left_part = (columns[None, :] == element[:, None]).astype(jnp.float32) * (1.0 - fraction)[
        :, None
    ]
    right_part = (columns[None, :] == element[:, None] + 1).astype(jnp.float32) * fraction[:, None]
    return left_part + right_part


def smooth(values, direction):
    extent = values.shape[direction]
    lower = lax.slice_in_dim(values, 0, extent - 2, axis=direction)
    middle = lax.slice_in_dim(values, 1, extent - 1, axis=direction)
    upper = lax.slice_in_dim(values, 2, extent, axis=direction)
    return (lower + 4.0 * middle + upper) / 6.0


def differ(values, direction):
    extent = values.shape[direction]
    lower = lax.slice_in_dim(values, 0, extent - 2, axis=direction)
    upper = lax.slice_in_dim(values, 2, extent, axis=direction)
    return 0.5 * (upper - lower)


def gradients(window):
    smooth_z = smooth(window, 2)
    slope_x = differ(smooth(smooth_z, 1), 0)
    slope_y = smooth(differ(smooth_z, 1), 0)
    slope_z = smooth(smooth(differ(window, 2), 1), 0)
    return jnp.stack([slope_x, slope_y, slope_z])


def interpolate(local_nodes, hat_y, hat_z):
    highest = lax.Precision.HIGHEST
    partial_z = jnp.einsum("cijk,zk->cijz", local_nodes, hat_z, precision=highest)
    return jnp.einsum("cijz,yj->ciyz", partial_z, hat_y, precision=highest)


def expand_x(partial_y, hat_x):
    return sum(
        hat_x[None, :, i, None, None] * partial_y[:, i, None] for i in range(hat_x.shape[1])
    )


def restrict(terms, hat_x, hat_y, hat_z):
    highest = lax.Precision.HIGHEST
    partial_x = jnp.stack(
        [jnp.sum(terms * hat_x[None, :, i, None, None], axis=1) for i in range(hat_x.shape[1])],
        axis=1,
    )
    partial_y = jnp.einsum("ciyz,yj->cijz", partial_x, hat_y, precision=highest)
    return jnp.einsum("cijz,zk->cijk", partial_y, hat_z, precision=highest)


def scatter_matrix(bricks, elements):
    columns = jnp.arange(bricks * elements + 1, dtype=jnp.int32)
    starts = jnp.arange(bricks, dtype=jnp.int32)[:, None] * elements
    rows = starts + jnp.arange(elements + 1, dtype=jnp.int32)[None, :]
    return (rows[:, :, None] == columns[None, None, :]).astype(jnp.float32)


def allsum(values):
    for axis in ("dev", "grp"):
        devices = lax.axis_size(axis)
        assert devices & (devices - 1) == 0
        step = 1
        while step < devices:
            pairs = [(i, i ^ step) for i in range(devices)]
            values = values + lax.ppermute(values, axis, pairs)
            step *= 2
    return values


def share_nodes(slab):
    for axis, dim in (("dev", 1), ("grp", 3)):
        devices, length = (lax.axis_size(axis), slab.shape[dim])
        up = [(i, i + 1) for i in range(devices - 1)]
        down = [(j, i) for i, j in up]
        last = lax.index_in_dim(slab, length - 1, axis=dim, keepdims=False)
        first = lax.index_in_dim(slab, 0, axis=dim, keepdims=False)
        before = lax.ppermute(last, axis, up)
        after = lax.ppermute(first, axis, down)
        head = lax.index_in_dim(slab, 0, axis=dim) + jnp.expand_dims(before, dim)
        tail = lax.index_in_dim(slab, length - 1, axis=dim) + jnp.expand_dims(after, dim)
        middle = lax.slice_in_dim(slab, 1, length - 1, axis=dim)
        slab = jnp.concatenate([head, middle, tail], axis=dim)
    return slab


def assemble(gathered):
    groups, bricks, comps, nbx, nby, nbz = gathered.shape
    highest = lax.Precision.HIGHEST
    place_x = scatter_matrix(bricks, nbx - 1)
    place_z = scatter_matrix(groups, nbz - 1)
    along_x = jnp.einsum("pqcijk,qix->pcxjk", gathered, place_x, precision=highest)
    return jnp.einsum("pcxjk,pkz->cxjz", along_x, place_z, precision=highest)


def local(ref_volume, def_volume, shifts, init_disp, precond):
    width_x, rows_y, depth_z = ref_volume.shape
    dev_count = lax.axis_size("dev")
    grp_count = lax.axis_size("grp")
    grp_index = lax.axis_index("grp")
    dev_index = lax.axis_index("dev")
    voxel_count = float(width_x * rows_y * depth_z * dev_count * grp_count)
    margin = SMAX + 1
    offset = shifts[0, 0]
    widened = with_halo(def_volume, (("dev", 0),), margin)
    up = [(i, i + 1) for i in range(grp_count - 1)]
    down = [(j, i) for i, j in up]
    below = lax.ppermute(widened[:, :, -1:], "grp", up)
    above = lax.ppermute(widened[:, :, :1], "grp", down)
    target = ref_volume.astype(jnp.float32)
    elements_x = width_x // E
    elements_z = depth_z // E
    nodes_y = rows_y // E + 1
    hat_x = hat_matrix(width_x, elements_x + 1)
    hat_y = hat_matrix(rows_y, nodes_y)
    hat_z = hat_matrix(depth_z, elements_z + 1)
    corner = (0, dev_index * elements_x, 0, grp_index * elements_z)
    extent = (3, elements_x + 1, nodes_y, elements_z + 1)
    local_nodes = lax.dynamic_slice(init_disp, corner, extent)
    local_precond = lax.dynamic_slice(precond, corner, extent)
    target_sums = jnp.stack([jnp.sum(target), jnp.sum(target * target)])
    partial = interpolate(local_nodes, hat_y, hat_z)
    slopes, warped, moments = native_slopes(
        offset.reshape(1), widened, below, above, partial, width_x
    )
    residual = target
    total_slab = None
    mean_ref = var_ref = None
    for iteration in range(ITERS):
        if iteration == 0:
            image_sums = jnp.sum(moments, axis=(1, 2))
        else:
            moved = interpolate(local_nodes, hat_y, hat_z)
            shift_field = expand_x(moved - partial, hat_x)
            warped = warped + jnp.sum(shift_field * slopes, axis=0)
            partial = moved
            image_sums = jnp.stack([jnp.sum(warped), jnp.sum(warped * warped)])
        if iteration == 0:
            sums = allsum(jnp.concatenate([target_sums, image_sums]))
            mean_ref = sums[0] / voxel_count
            var_ref = sums[1] / voxel_count - mean_ref * mean_ref
            image_sums = sums[2:]
        else:
            image_sums = allsum(image_sums)
        mean_img = image_sums[0] / voxel_count
        var_img = image_sums[1] / voxel_count - mean_img * mean_img
        ratio = jnp.sqrt((var_ref + epsilon) / (var_img + epsilon))
        residual = target - mean_ref - ratio * (warped - mean_img)
        slab = restrict(slopes * residual[None], hat_x, hat_y, hat_z)
        total_slab = slab if total_slab is None else total_slab + slab
        if iteration + 1 < ITERS:
            local_nodes = local_nodes + local_precond * share_nodes(slab)
    squares = jnp.sum(residual * residual)
    packed = jnp.concatenate([total_slab.reshape(-1), squares[None]])
    gathered = lax.all_gather(packed.reshape(2, -1), ("grp", "dev")).reshape(grp_count * dev_count, -1)
    pieces = gathered[:, :-1].reshape((grp_count, dev_count) + total_slab.shape)
    forces = assemble(pieces)
    motion = init_disp + precond * forces
    misfit = jnp.sqrt(jnp.sum(gathered[:, -1]) / voxel_count)
    return (motion, residual, misfit)


def solution(mesh):
    placed = (P("dev", None, "grp"), P("dev", None, "grp"), P("grp", "dev"), P(), P())
    return jax.shard_map(
        local,
        mesh=mesh,
        in_specs=placed,
        out_specs=(P(), P("dev", None, "grp"), P()),
        check_vma=False,
    )
```

```python
import jax
import jax.numpy as jnp
from jax import lax
from jax.sharding import PartitionSpec as P
from jax.experimental import pallas as pl
from jax.experimental.pallas import tpu as pltpu

E = 16
SMAX = 8
ITERS = 2


epsilon = 1e-06


def with_halo(shard, sides, width):
    for axis, dim in sides:
        devices, length = (lax.axis_size(axis), shard.shape[dim])
        up = [(i, (i + 1) % devices) for i in range(devices - 1)]
        down = [(j, i) for i, j in up]
        last = lax.slice_in_dim(shard, length - width, length, axis=dim)
        initial = lax.slice_in_dim(shard, 0, width, axis=dim)
        before = lax.ppermute(last, axis, up)
        after = lax.ppermute(initial, axis, down)
        shard = jnp.concatenate([before, shard, after], axis=dim)
    return shard


from jax.experimental import pallas as pl
from jax.experimental.pallas import tpu as pltpu

PLANES = 8


def _native_kernel(offset_ref, w_ref, lo_ref, hi_ref, sl_ref, keep_ref):
    step = pl.program_id(0)
    _, wy, wz = w_ref.shape
    row = lax.broadcasted_iota(jnp.int32, (wy, wz), 0)
    lane = lax.broadcasted_iota(jnp.int32, (wy, wz), 1)
    sixth = 1.0 / 6.0
    base = offset_ref[0] + SMAX + step * PLANES

    def planes(t):
        p = base + t
        w = w_ref[p].astype(jnp.float32)
        below = jnp.where(lane == 0, lo_ref[p].astype(jnp.float32), pltpu.roll(w, 1, 1))
        above = jnp.where(lane == wz - 1, hi_ref[p].astype(jnp.float32), pltpu.roll(w, wz - 1, 1))
        smooth_z = (below + 4.0 * w + above) * sixth
        differ_z = 0.5 * (above - below)
        s_lo = jnp.where(row == 0, 0.0, pltpu.roll(smooth_z, 1, 0))
        s_hi = jnp.where(row == wy - 1, 0.0, pltpu.roll(smooth_z, wy - 1, 0))
        d_lo = jnp.where(row == 0, 0.0, pltpu.roll(differ_z, 1, 0))
        d_hi = jnp.where(row == wy - 1, 0.0, pltpu.roll(differ_z, wy - 1, 0))
        return (
            (s_lo + 4.0 * smooth_z + s_hi) * sixth,
            0.5 * (s_hi - s_lo),
            (d_lo + 4.0 * differ_z + d_hi) * sixth,
            w,
        )

    @pl.when(step == 0)
    def _():
        for t in range(2):
            for n, value in enumerate(planes(t)):
                keep_ref[t, n] = value

    window = [tuple(keep_ref[t, n] for n in range(4)) for t in range(2)]
    for k in range(PLANES):
        window.append(planes(k + 2))
        prev, mid, nxt = window[k], window[k + 1], window[k + 2]
        sl_ref[0, k] = 0.5 * (nxt[0] - prev[0])
        sl_ref[1, k] = (prev[1] + 4.0 * mid[1] + nxt[1]) * sixth
        sl_ref[2, k] = (prev[2] + 4.0 * mid[2] + nxt[2]) * sixth
    for t in range(2):
        for n, value in enumerate(window[PLANES + t]):
            keep_ref[t, n] = value


def native_slopes(offset, widened, below, above, width_x, interpret=False):
    _, wy, wz = widened.shape
    assert width_x % PLANES == 0
    whole = pl.BlockSpec(widened.shape, lambda i, o: (0, 0, 0))
    face = pl.BlockSpec(below.shape, lambda i, o: (0, 0, 0))
    spec = pltpu.PrefetchScalarGridSpec(
        num_scalar_prefetch=1,
        grid=(width_x // PLANES,),
        in_specs=[whole, face, face],
        scratch_shapes=[pltpu.VMEM((2, 4, wy, wz), jnp.float32)],
        out_specs=[
            pl.BlockSpec((3, PLANES, wy, wz), lambda i, o: (0, i, 0, 0)),
        ],
    )
    return pl.pallas_call(
        _native_kernel,
        grid_spec=spec,
        out_shape=[
            jax.ShapeDtypeStruct((3, width_x, wy, wz), jnp.float32),
        ],
        interpret=interpret,
    )(offset, widened, below, above)


def hat_matrix(voxels, nodes):
    positions = jnp.arange(voxels, dtype=jnp.int32)
    element = positions // E
    fraction = (positions - element * E).astype(jnp.float32) / E
    columns = jnp.arange(nodes, dtype=jnp.int32)
    left_part = (columns[None, :] == element[:, None]).astype(jnp.float32) * (1.0 - fraction)[
        :, None
    ]
    right_part = (columns[None, :] == element[:, None] + 1).astype(jnp.float32) * fraction[:, None]
    return left_part + right_part


def smooth(values, direction):
    extent = values.shape[direction]
    lower = lax.slice_in_dim(values, 0, extent - 2, axis=direction)
    middle = lax.slice_in_dim(values, 1, extent - 1, axis=direction)
    upper = lax.slice_in_dim(values, 2, extent, axis=direction)
    return (lower + 4.0 * middle + upper) / 6.0


def differ(values, direction):
    extent = values.shape[direction]
    lower = lax.slice_in_dim(values, 0, extent - 2, axis=direction)
    upper = lax.slice_in_dim(values, 2, extent, axis=direction)
    return 0.5 * (upper - lower)


def gradients(window):
    smooth_z = smooth(window, 2)
    slope_x = differ(smooth(smooth_z, 1), 0)
    slope_y = smooth(differ(smooth_z, 1), 0)
    slope_z = smooth(smooth(differ(window, 2), 1), 0)
    return jnp.stack([slope_x, slope_y, slope_z])


def interpolate(local_nodes, hat_y, hat_z):
    highest = lax.Precision.HIGHEST
    partial_z = jnp.einsum("cijk,zk->cijz", local_nodes, hat_z, precision=highest)
    return jnp.einsum("cijz,yj->ciyz", partial_z, hat_y, precision=highest)


def expand_x(partial_y, hat_x):
    return sum(
        hat_x[None, :, i, None, None] * partial_y[:, i, None] for i in range(hat_x.shape[1])
    )


def restrict(terms, hat_x, hat_y, hat_z):
    highest = lax.Precision.HIGHEST
    partial_x = jnp.stack(
        [jnp.sum(terms * hat_x[None, :, i, None, None], axis=1) for i in range(hat_x.shape[1])],
        axis=1,
    )
    partial_y = jnp.einsum("ciyz,yj->cijz", partial_x, hat_y, precision=highest)
    return jnp.einsum("cijz,zk->cijk", partial_y, hat_z, precision=highest)


def scatter_matrix(bricks, elements):
    columns = jnp.arange(bricks * elements + 1, dtype=jnp.int32)
    starts = jnp.arange(bricks, dtype=jnp.int32)[:, None] * elements
    rows = starts + jnp.arange(elements + 1, dtype=jnp.int32)[None, :]
    return (rows[:, :, None] == columns[None, None, :]).astype(jnp.float32)


def allsum(values):
    for axis in ("dev", "grp"):
        devices = lax.axis_size(axis)
        assert devices & (devices - 1) == 0
        step = 1
        while step < devices:
            pairs = [(i, i ^ step) for i in range(devices)]
            values = values + lax.ppermute(values, axis, pairs)
            step *= 2
    return values


def share_nodes(slab):
    for axis, dim in (("dev", 1), ("grp", 3)):
        devices, length = (lax.axis_size(axis), slab.shape[dim])
        up = [(i, i + 1) for i in range(devices - 1)]
        down = [(j, i) for i, j in up]
        last = lax.index_in_dim(slab, length - 1, axis=dim, keepdims=False)
        first = lax.index_in_dim(slab, 0, axis=dim, keepdims=False)
        before = lax.ppermute(last, axis, up)
        after = lax.ppermute(first, axis, down)
        head = lax.index_in_dim(slab, 0, axis=dim) + jnp.expand_dims(before, dim)
        tail = lax.index_in_dim(slab, length - 1, axis=dim) + jnp.expand_dims(after, dim)
        middle = lax.slice_in_dim(slab, 1, length - 1, axis=dim)
        slab = jnp.concatenate([head, middle, tail], axis=dim)
    return slab


def assemble(gathered):
    groups, bricks, comps, nbx, nby, nbz = gathered.shape
    highest = lax.Precision.HIGHEST
    place_x = scatter_matrix(bricks, nbx - 1)
    place_z = scatter_matrix(groups, nbz - 1)
    along_x = jnp.einsum("pqcijk,qix->pcxjk", gathered, place_x, precision=highest)
    return jnp.einsum("pcxjk,pkz->cxjz", along_x, place_z, precision=highest)


def local(ref_volume, def_volume, shifts, init_disp, precond):
    width_x, rows_y, depth_z = ref_volume.shape
    dev_count = lax.axis_size("dev")
    grp_count = lax.axis_size("grp")
    grp_index = lax.axis_index("grp")
    dev_index = lax.axis_index("dev")
    voxel_count = float(width_x * rows_y * depth_z * dev_count * grp_count)
    margin = SMAX + 1
    offset = shifts[0, 0]
    widened = with_halo(def_volume, (("dev", 0),), margin)
    up = [(i, i + 1) for i in range(grp_count - 1)]
    down = [(j, i) for i, j in up]
    below = lax.ppermute(widened[:, :, -1:], "grp", up)
    above = lax.ppermute(widened[:, :, :1], "grp", down)
    (slopes,) = native_slopes(offset.reshape(1), widened, below, above, width_x)
    sample = lax.dynamic_slice_in_dim(widened, offset + margin, width_x, 0).astype(jnp.float32)
    target = ref_volume.astype(jnp.float32)
    elements_x = width_x // E
    elements_z = depth_z // E
    nodes_y = rows_y // E + 1
    hat_x = hat_matrix(width_x, elements_x + 1)
    hat_y = hat_matrix(rows_y, nodes_y)
    hat_z = hat_matrix(depth_z, elements_z + 1)
    corner = (0, dev_index * elements_x, 0, grp_index * elements_z)
    extent = (3, elements_x + 1, nodes_y, elements_z + 1)
    local_nodes = lax.dynamic_slice(init_disp, corner, extent)
    local_precond = lax.dynamic_slice(precond, corner, extent)
    target_sums = jnp.stack([jnp.sum(target), jnp.sum(target * target)])
    residual = target
    total_slab = None
    mean_ref = var_ref = None
    for iteration in range(ITERS):
        shift_field = expand_x(interpolate(local_nodes, hat_y, hat_z), hat_x)
        warped = sample + jnp.sum(shift_field * slopes, axis=0)
        image_sums = jnp.stack([jnp.sum(warped), jnp.sum(warped * warped)])
        if iteration == 0:
            sums = allsum(jnp.concatenate([target_sums, image_sums]))
            mean_ref = sums[0] / voxel_count
            var_ref = sums[1] / voxel_count - mean_ref * mean_ref
            image_sums = sums[2:]
        else:
            image_sums = allsum(image_sums)
        mean_img = image_sums[0] / voxel_count
        var_img = image_sums[1] / voxel_count - mean_img * mean_img
        ratio = jnp.sqrt((var_ref + epsilon) / (var_img + epsilon))
        residual = target - mean_ref - ratio * (warped - mean_img)
        slab = restrict(slopes * residual[None], hat_x, hat_y, hat_z)
        total_slab = slab if total_slab is None else total_slab + slab
        if iteration + 1 < ITERS:
            local_nodes = local_nodes + local_precond * share_nodes(slab)
    squares = jnp.sum(residual * residual)
    packed = jnp.concatenate([total_slab.reshape(-1), squares[None]])
    gathered = lax.all_gather(packed.reshape(2, -1), ("grp", "dev")).reshape(grp_count * dev_count, -1)
    pieces = gathered[:, :-1].reshape((grp_count, dev_count) + total_slab.shape)
    forces = assemble(pieces)
    motion = init_disp + precond * forces
    misfit = jnp.sqrt(jnp.sum(gathered[:, -1]) / voxel_count)
    return (motion, residual, misfit)


def solution(mesh):
    placed = (P("dev", None, "grp"), P("dev", None, "grp"), P("grp", "dev"), P(), P())
    return jax.shard_map(
        local,
        mesh=mesh,
        in_specs=placed,
        out_specs=(P(), P("dev", None, "grp"), P()),
        check_vma=False,
    )
```
